1024 devices in a mesh: dp: 2 (over x_hi), expert: 32 (over y, x_lo), fsdp: 16 (over z, core).
Axes of the slice: x: 8 (x_hi: 2, x_lo: 4; x = x_hi * 4 + x_lo), y: 8, z: 8, core: 2. Of those that a mesh axis runs over, the one named last changes fastest.
Arguments:
- tokens: bfloat16 [2048, 2048], P(('dp', 'expert'), 'fsdp'), may hold values from -6 to 6
- grad_out: bfloat16 [2048, 2048], P(('dp', 'expert'), 'fsdp'), may hold values from -6 to 6
- expert_ids: int32 [2048, 6], P(('dp', 'expert')), may hold values from 0 to 63, all different within a row; in each aligned block of 32 rows (0 to 31, 32 to 63, ...) at most 3 rows name the same one
- gate_weights: float32 [2048, 6], P(('dp', 'expert')), may hold values from 0.05 to 1
- w_gate: bfloat16 [64, 1408, 2048], P('expert', 'fsdp'), may hold values from -0.125 to 0.125
- w_up: bfloat16 [64, 1408, 2048], P('expert', 'fsdp'), may hold values from -0.125 to 0.125
- w_down: bfloat16 [64, 1408, 2048], P('expert', None, 'fsdp'), may hold values from -0.15625 to 0.15625
Outputs:
- mixed: bfloat16 [2048, 2048], P(('dp', 'expert'), 'fsdp')
- grad_tokens: bfloat16 [2048, 2048], P(('dp', 'expert'), 'fsdp')
- grad_w_gate: bfloat16 [64, 1408, 2048], P('expert', 'fsdp', 'dp')
- grad_w_up: bfloat16 [64, 1408, 2048], P('expert', 'fsdp', 'dp')
- grad_w_down: bfloat16 [64, 1408, 2048], P('expert', 'dp', 'fsdp')
The draws below stay inside these ranges and needn't reach their ends.
Inputs may be any that keep to these rules, and one draw needn't show every extreme that they name: `expert_ids`: in each aligned block of 32 rows (the tokens of one index of dp and expert) no expert is named by more than 3 rows, a bound that some block reaches; a row names distinct experts.
All inputs are finite; a program needn't handle non-finite values.
Results may differ from the reference program's by a relative error of at most 0.025.
Values may be sent and summed in bfloat16 or wider, within the bound.
No kernel may reach another device: no remote copies, remote signals or barrier semaphores. Data moves between devices by JAX's collectives and lax.ppermute only.
A program may use at most 32 MiB of HBM per device.

```python
import math
import jax
import jax.numpy as jnp
import numpy as np
from jax import lax

D = 2048
FF = 1408
TOPK = 6
TOK_G = 32
EXPERTS = 64
TOKENS = 2048
CAP = 3
N_DP = 2
N_EXPERT = 32
N_FSDP = 16


def steps_of(key, dims, split, least, top_value):
    factor_of = 1.0
    for axis_at, parts in split:
        draws = jax.random.uniform(jax.random.fold_in(jax.random.fold_in(key, 6), axis_at), (parts,), jnp.float32, least / len(split), top_value / len(split))
        factor_of = factor_of * jnp.repeat(jnp.exp(draws), dims[axis_at] // parts).reshape((-1,) + (1,) * (len(dims) - 1 - axis_at))
    return factor_of


def deal_out(rng, own, number, rows, count, top, most, skew):
    sequence = jax.random.permutation(rng, count)
    crowded, usual = portions_of(count, rows * top, most, skew, True), portions_of(count, rows * top, most, skew, False)
    places = jnp.arange(count)

    def named(lengths, offset_by):
        used = int((lengths > 0).sum())
        fixed = max(1, used // 4)
        passed = fixed + (places - fixed + offset_by * (used - fixed)) % max(1, count - fixed)
        return jnp.zeros((count,), jnp.int32).at[sequence[jnp.where(places < fixed, places, passed)]].set(jnp.asarray(lengths, jnp.int32))

    lengths = jnp.where(number % 4 == 0, named(crowded, number // 4), named(usual, number - number // 4 - 1))
    mixed = jax.random.permutation(jax.random.fold_in(own, 3), count)
    giver, receiver = mixed[0:count // 2 * 2:2], mixed[1:count // 2 * 2:2]
    slack = jnp.minimum(lengths[giver] - 1, most - lengths[receiver]) // 2
    slack = jnp.where((giver == sequence[0]) | (receiver == sequence[0]) | (lengths[receiver] == 0), 0, jnp.maximum(slack, 0))
    passed = jax.random.randint(jax.random.fold_in(own, 4), (count // 2,), 0, 1 << 20) % (slack + 1)
    lengths = lengths.at[giver].add(-passed).at[receiver].add(passed)
    labels = jnp.searchsorted(jnp.cumsum(lengths), jnp.arange(rows * top), side="right").astype(jnp.int32)
    grid = labels.reshape(top, rows).T
    grid = grid[jax.random.permutation(jax.random.fold_in(own, 1), rows)]
    offset_by = jax.random.randint(jax.random.fold_in(own, 2), (rows, 1), 0, top)
    return jnp.take_along_axis(grid, (jnp.arange(top)[None, :] + offset_by) % top, axis=1)


def portions_of(count, total, most, skew, full):
    weights = [(1 << 20) // math.isqrt(standing ** skew) + 1 for standing in range(1, count + 1)]
    largest = most if full else min(most, max(-(-total // count), total * weights[0] // sum(weights)))
    least = 1 if total - largest >= count - 1 else 0
    counts, spare = [largest] + [least] * (count - 1), total - largest - least * (count - 1)
    while spare > 0:
        free = [i for i in range(1, count) if counts[i] < largest] or [i for i in range(1, count) if counts[i] < most]
        mass, budget = sum([weights[i] for i in free]), spare
        for i in free:
            more = min(most - counts[i], max(1, budget * weights[i] // mass), spare)
            counts[i] = counts[i] + more
            spare = spare - more
    return np.array(counts)


def bell_draw(stream_key, extent, width, limit, cuts=(), held_as=jnp.bfloat16):
    array = jax.random.normal(stream_key, extent, jnp.float32) * width
    if len(cuts) > 0:
        array = steps_of(stream_key, extent, cuts, -0.22, 0.18) * array
    return jnp.clip(array, min=-limit, max=limit).astype(held_as)


def setup_inputs(seed: int = 0) -> dict:
    arg_keys = jax.random.split(jax.random.key(seed), 8)
    tokens = bell_draw(arg_keys[0], (TOKENS, D), 1.0, 6.0, ((0, 64), (1, 16)))
    grad_out = bell_draw(arg_keys[1], (TOKENS, D), 1.0, 6.0, ((0, 64), (1, 16)))
    expert_ids_keys = jax.random.split(jax.random.fold_in(arg_keys[2], 1), TOKENS // TOK_G)
    expert_ids_turns = jax.random.permutation(jax.random.fold_in(arg_keys[2], 3), TOKENS // TOK_G)
    expert_ids = jax.vmap(lambda own, number: deal_out(jax.random.fold_in(arg_keys[2], 2), own, number, TOK_G, EXPERTS, TOPK, CAP, 2))(expert_ids_keys, expert_ids_turns).reshape((TOKENS, TOPK))
    gate_weights = jnp.clip(jnp.exp(math.log(1.0) - 2.9957323 * jax.random.uniform(arg_keys[3], (TOKENS, TOPK), jnp.float32) ** steps_of(arg_keys[3], (TOKENS, TOPK), ((0, 64),), -0.2, 0.2)), 0.05, 1.0)
    w_gate = bell_draw(arg_keys[4], (EXPERTS, FF, D), D ** -0.5, 0.125, ((0, 32), (1, 16)))
    w_up = bell_draw(arg_keys[5], (EXPERTS, FF, D), D ** -0.5, 0.125, ((0, 32), (1, 16)))
    w_down = bell_draw(arg_keys[6], (EXPERTS, FF, D), FF ** -0.5, 0.15625, ((0, 32), (2, 16)))
    return {"tokens": tokens, "grad_out": grad_out, "expert_ids": expert_ids, "gate_weights": gate_weights, "w_gate": w_gate, "w_up": w_up, "w_down": w_down}


def rounded(values):
    return lax.optimization_barrier(values.astype(jnp.bfloat16)).astype(jnp.float32)


def silu_parts(pre_act):
    sigmoid_value = jax.nn.sigmoid(pre_act)
    return pre_act * sigmoid_value, sigmoid_value * (1.0 + pre_act * (1.0 - sigmoid_value))


def reference(tokens, grad_out, expert_ids, gate_weights, w_gate, w_up, w_down):
    blocks = N_DP * N_EXPERT
    per_block = TOK_G * TOPK
    route_ids = expert_ids.reshape(blocks, per_block)
    onehot = (route_ids[:, :, None] == jnp.arange(EXPERTS, dtype=jnp.int32)[None, None, :]).astype(jnp.int32)
    before = jnp.cumsum(onehot, axis=1) - onehot
    slot_rank = jnp.sum(before * onehot, axis=2)
    block_ids = jnp.arange(blocks, dtype=jnp.int32)[:, None]
    rows_each = blocks * CAP
    where_to = (route_ids * rows_each + block_ids * CAP + slot_rank).reshape(-1).astype(jnp.int32)
    token_of = (block_ids * TOK_G + jnp.arange(per_block, dtype=jnp.int32)[None, :] // TOPK).reshape(-1).astype(jnp.int32)
    table_size = EXPERTS * rows_each
    slot_token = jnp.zeros((table_size,), jnp.int32).at[where_to].set(token_of).reshape(EXPERTS, rows_each)
    slot_gate = jnp.zeros((table_size,), jnp.float32).at[where_to].set(gate_weights.reshape(-1)).reshape(EXPERTS, rows_each)
    slot_alive = jnp.zeros((table_size,), jnp.float32).at[where_to].set(1.0).reshape(EXPERTS, rows_each)
    feature_group = D // N_FSDP
    hidden_group = FF // N_FSDP
    group_rows = N_EXPERT * CAP

    def per_expert(inputs):
        slot_rows, slot_gates, alive, weight_gate, weight_up, weight_down = inputs
        alive_mask = alive[:, None] > 0.5
        x_rows = jnp.where(alive_mask, tokens[slot_rows], jnp.zeros((), jnp.bfloat16))
        gate_pre = jnp.dot(x_rows, weight_gate.T, preferred_element_type=jnp.float32)
        up_pre = jnp.dot(x_rows, weight_up.T, preferred_element_type=jnp.float32)
        activation, slope_term = silu_parts(gate_pre)
        hidden = (activation * up_pre).astype(jnp.bfloat16)
        expert_out = jnp.dot(hidden, weight_down, preferred_element_type=jnp.float32).astype(jnp.bfloat16)
        scaled_grad = jnp.where(alive_mask, slot_gates[:, None] * grad_out[slot_rows].astype(jnp.float32), 0.0).astype(jnp.bfloat16)
        hidden_parts = jnp.einsum("rgd,fgd->grf", scaled_grad.reshape(-1, N_FSDP, feature_group).astype(jnp.float32),
                                  weight_down.reshape(FF, N_FSDP, feature_group).astype(jnp.float32))
        grad_hidden = jnp.sum(rounded(hidden_parts), axis=0)
        grad_gate_pre = (grad_hidden * up_pre * slope_term).astype(jnp.bfloat16)
        grad_up_pre = (grad_hidden * activation).astype(jnp.bfloat16)
        input_parts = jnp.einsum("rgf,gfd->grd", grad_gate_pre.reshape(-1, N_FSDP, hidden_group).astype(jnp.float32),
                                 weight_gate.reshape(N_FSDP, hidden_group, D).astype(jnp.float32))
        input_parts = input_parts + jnp.einsum("rgf,gfd->grd", grad_up_pre.reshape(-1, N_FSDP, hidden_group).astype(jnp.float32),
                                               weight_up.reshape(N_FSDP, hidden_group, D).astype(jnp.float32))
        input_grad = jnp.sum(rounded(input_parts), axis=0).astype(jnp.bfloat16)
        x_groups = x_rows.reshape(N_DP, group_rows, D).astype(jnp.float32)
        grad_groups = scaled_grad.reshape(N_DP, group_rows, D).astype(jnp.float32)
        grad_gate_w = jnp.sum(rounded(jnp.einsum("prf,prd->pfd", grad_gate_pre.reshape(N_DP, group_rows, FF).astype(jnp.float32), x_groups)), axis=0)
        grad_up_w = jnp.sum(rounded(jnp.einsum("prf,prd->pfd", grad_up_pre.reshape(N_DP, group_rows, FF).astype(jnp.float32), x_groups)), axis=0)
        grad_down_w = jnp.sum(rounded(jnp.einsum("prf,prd->pfd", hidden.reshape(N_DP, group_rows, FF).astype(jnp.float32), grad_groups)), axis=0)
        return (expert_out, input_grad, grad_gate_w.astype(jnp.bfloat16),
                grad_up_w.astype(jnp.bfloat16), grad_down_w.astype(jnp.bfloat16))

    expert_out, input_grad, grad_w_gate, grad_w_up, grad_w_down = lax.map(
        per_expert, (slot_token, slot_gate, slot_alive, w_gate, w_up, w_down))
    flat_tokens = slot_token.reshape(-1)
    weighted_out = expert_out.reshape(-1, D).astype(jnp.float32) * slot_gate.reshape(-1, 1)
    mixed = jnp.zeros((TOKENS, D), jnp.float32).at[flat_tokens].add(weighted_out).astype(jnp.bfloat16)
    alive_grad = input_grad.reshape(-1, D).astype(jnp.float32) * slot_alive.reshape(-1, 1)
    grad_tokens = jnp.zeros((TOKENS, D), jnp.float32).at[flat_tokens].add(alive_grad).astype(jnp.bfloat16)
    return mixed, grad_tokens, grad_w_gate, grad_w_up, grad_w_down
```

```python
import jax
import jax.numpy as jnp
from jax import lax
from jax.sharding import PartitionSpec as P


def rounded(values):
    return lax.optimization_barrier(values.astype(jnp.bfloat16)).astype(jnp.float32)


def silu_parts(pre_act):
    sigmoid_value = jax.nn.sigmoid(pre_act)
    return (pre_act * sigmoid_value, sigmoid_value * (1.0 + pre_act * (1.0 - sigmoid_value)))


def dp_reduce(part, axis):
    groups = lax.axis_size("dp")
    if groups != 2:
        return lax.psum_scatter(part, "dp", scatter_dimension=axis, tiled=True)
    me = lax.axis_index("dp")
    halves = jnp.stack(jnp.split(part, 2, axis=axis))
    keep = lax.dynamic_index_in_dim(halves, me, 0, keepdims=False)
    send = lax.dynamic_index_in_dim(halves, 1 - me, 0, keepdims=False)
    got = lax.ppermute(send, "dp", perm=[(0, 1), (1, 0)])
    return (keep.astype(jnp.float32) + got.astype(jnp.float32)).astype(jnp.bfloat16)


def body(tokens, grad_out, expert_ids, gate_weights, w_gate, w_up, w_down):
    tok_rows = tokens.shape[0]
    choose = expert_ids.shape[1]
    exp_local = w_gate.shape[0]
    model_width = w_gate.shape[2]
    owners = lax.axis_size("expert")
    experts_all = owners * exp_local
    capacity = max(2, min(tok_rows, 5 * choose * tok_rows // (4 * experts_all)))
    slot_count = experts_all * capacity
    flat_ids = expert_ids.reshape(-1)
    onehot = (flat_ids[:, None] == jnp.arange(experts_all, dtype=jnp.int32)[None, :]).astype(
        jnp.int32
    )
    before = jnp.cumsum(onehot, axis=0) - onehot
    slot_rank = jnp.sum(before * onehot, axis=1)
    slot_of = (flat_ids * capacity + slot_rank).reshape(tok_rows, choose)
    placed = (slot_of[:, :, None] == jnp.arange(slot_count, dtype=jnp.int32)[None, None, :]).astype(
        jnp.float32
    )
    picker = jnp.sum(placed, axis=1).T
    weighted = jnp.einsum("tks,tk->st", placed, gate_weights, precision=lax.Precision.HIGHEST)
    picker_half = picker.astype(jnp.bfloat16)
    scaled_grad = jnp.dot(
        weighted, grad_out.astype(jnp.float32), precision=lax.Precision.HIGHEST
    ).astype(jnp.bfloat16)
    full_rows = lax.all_gather(tokens, "fsdp", axis=1, tiled=True)
    outgoing = jnp.dot(picker_half, full_rows, preferred_element_type=jnp.float32).astype(
        jnp.bfloat16
    )
    both_in = lax.all_to_all(
        jnp.concatenate([outgoing, scaled_grad], axis=1),
        "expert", split_axis=0, concat_axis=0, tiled=True,
    )
    rows_in, grads_in = both_in[:, :model_width], both_in[:, model_width:]
    received = rows_in.reshape(owners, exp_local, capacity, model_width)
    cotangent = grads_in.reshape(owners, exp_local, capacity, -1)
    gate_pre = jnp.einsum("jecd,efd->jecf", received, w_gate, preferred_element_type=jnp.float32)
    up_pre = jnp.einsum("jecd,efd->jecf", received, w_up, preferred_element_type=jnp.float32)
    activation, slope_term = silu_parts(gate_pre)
    hidden = (activation * up_pre).astype(jnp.bfloat16)
    hidden_all = lax.all_gather(hidden, "fsdp", axis=3, tiled=True)
    expert_out = jnp.einsum(
        "jecf,efd->jecd", hidden_all, w_down, preferred_element_type=jnp.float32
    ).astype(jnp.bfloat16)
    hidden_parts = rounded(
        jnp.einsum("jecd,efd->jecf", cotangent, w_down, preferred_element_type=jnp.float32)
    )
    grad_hidden = lax.psum_scatter(
        hidden_parts.astype(jnp.bfloat16), "fsdp", scatter_dimension=3, tiled=True
    ).astype(jnp.float32)
    grad_gate_pre = (grad_hidden * up_pre * slope_term).astype(jnp.bfloat16)
    grad_up_pre = (grad_hidden * activation).astype(jnp.bfloat16)
    input_parts = jnp.einsum(
        "jecf,efd->jecd", grad_gate_pre, w_gate, preferred_element_type=jnp.float32
    )
    input_parts = rounded(
        input_parts
        + jnp.einsum("jecf,efd->jecd", grad_up_pre, w_up, preferred_element_type=jnp.float32)
    )
    input_slices = lax.psum_scatter(
        input_parts.astype(jnp.bfloat16), "fsdp", scatter_dimension=3, tiled=True
    )
    feat = input_slices.shape[-1]
    both_back = lax.all_to_all(
        jnp.concatenate(
            [expert_out.reshape(slot_count, -1), input_slices.reshape(slot_count, -1)], axis=1
        ),
        "expert", split_axis=0, concat_axis=0, tiled=True,
    )
    mixed_slots, input_slots = both_back[:, :feat], both_back[:, feat:]
    mixed = jnp.dot(
        weighted.T, mixed_slots.astype(jnp.float32), precision=lax.Precision.HIGHEST
    ).astype(jnp.bfloat16)
    grad_tokens = jnp.dot(
        picker.T, input_slots.astype(jnp.float32), precision=lax.Precision.HIGHEST
    ).astype(jnp.bfloat16)
    grad_gate_w = rounded(
        jnp.einsum("jecf,jecd->efd", grad_gate_pre, received, preferred_element_type=jnp.float32)
    )
    grad_up_w = rounded(
        jnp.einsum("jecf,jecd->efd", grad_up_pre, received, preferred_element_type=jnp.float32)
    )
    grad_down_w = rounded(
        jnp.einsum("jecf,jecd->efd", hidden_all, cotangent, preferred_element_type=jnp.float32)
    )
    summed_gate = dp_reduce(grad_gate_w.astype(jnp.bfloat16), 2).astype(jnp.float32)
    summed_up = dp_reduce(grad_up_w.astype(jnp.bfloat16), 2).astype(jnp.float32)
    summed_down = dp_reduce(grad_down_w.astype(jnp.bfloat16), 1)
    return (
        mixed,
        grad_tokens,
        summed_gate.astype(jnp.bfloat16),
        summed_up.astype(jnp.bfloat16),
        summed_down,
    )


def solution(mesh):
    in_specs = (
        P(("dp", "expert"), "fsdp"),
        P(("dp", "expert"), "fsdp"),
        P(("dp", "expert"), None),
        P(("dp", "expert"), None),
        P("expert", "fsdp", None),
        P("expert", "fsdp", None),
        P("expert", None, "fsdp"),
    )
    out_specs = (
        P(("dp", "expert"), "fsdp"),
        P(("dp", "expert"), "fsdp"),
        P("expert", "fsdp", "dp"),
        P("expert", "fsdp", "dp"),
        P("expert", "dp", "fsdp"),
    )
    return jax.shard_map(body, mesh=mesh, in_specs=in_specs, out_specs=out_specs, check_vma=False)
```

```python
import jax
import jax.numpy as jnp
from jax import lax
from jax.sharding import PartitionSpec as P


def rounded(values):
    return lax.optimization_barrier(values.astype(jnp.bfloat16)).astype(jnp.float32)


def silu_parts(pre_act):
    sigmoid_value = jax.nn.sigmoid(pre_act)
    return (pre_act * sigmoid_value, sigmoid_value * (1.0 + pre_act * (1.0 - sigmoid_value)))


def dp_reduce(part, axis):
    groups = lax.axis_size("dp")
    if groups != 2:
        return lax.psum_scatter(part, "dp", scatter_dimension=axis, tiled=True)
    me = lax.axis_index("dp")
    halves = jnp.stack(jnp.split(part, 2, axis=axis))
    keep = lax.dynamic_index_in_dim(halves, me, 0, keepdims=False)
    send = lax.dynamic_index_in_dim(halves, 1 - me, 0, keepdims=False)
    got = lax.ppermute(send, "dp", perm=[(0, 1), (1, 0)])
    return (keep.astype(jnp.float32) + got.astype(jnp.float32)).astype(jnp.bfloat16)


def body(tokens, grad_out, expert_ids, gate_weights, w_gate, w_up, w_down):
    tok_rows = tokens.shape[0]
    choose = expert_ids.shape[1]
    exp_local = w_gate.shape[0]
    model_width = w_gate.shape[2]
    owners = lax.axis_size("expert")
    experts_all = owners * exp_local
    capacity = max(2, min(tok_rows, 5 * choose * tok_rows // (4 * experts_all)))
    slot_count = experts_all * capacity
    flat_ids = expert_ids.reshape(-1)
    onehot = (flat_ids[:, None] == jnp.arange(experts_all, dtype=jnp.int32)[None, :]).astype(
        jnp.int32
    )
    before = jnp.cumsum(onehot, axis=0) - onehot
    slot_rank = jnp.sum(before * onehot, axis=1)
    slot_of = (flat_ids * capacity + slot_rank).reshape(tok_rows, choose)
    placed = (slot_of[:, :, None] == jnp.arange(slot_count, dtype=jnp.int32)[None, None, :]).astype(
        jnp.float32
    )
    picker = jnp.sum(placed, axis=1).T
    weighted = jnp.einsum("tks,tk->st", placed, gate_weights, precision=lax.Precision.HIGHEST)
    picker_half = picker.astype(jnp.bfloat16)
    scaled_grad = jnp.dot(
        weighted, grad_out.astype(jnp.float32), precision=lax.Precision.HIGHEST
    ).astype(jnp.bfloat16)
    full_rows = lax.all_gather(tokens, "fsdp", axis=1, tiled=True)
    outgoing = jnp.dot(picker_half, full_rows, preferred_element_type=jnp.float32).astype(
        jnp.bfloat16
    )
    both_in = lax.all_to_all(
        jnp.concatenate([outgoing, scaled_grad], axis=1),
        "expert", split_axis=0, concat_axis=0, tiled=True,
    )
    rows_in, grads_in = both_in[:, :model_width], both_in[:, model_width:]
    received = rows_in.reshape(owners, exp_local, capacity, model_width)
    cotangent = grads_in.reshape(owners, exp_local, capacity, -1)
    gate_pre = jnp.einsum("jecd,efd->jecf", received, w_gate, preferred_element_type=jnp.float32)
    up_pre = jnp.einsum("jecd,efd->jecf", received, w_up, preferred_element_type=jnp.float32)
    activation, slope_term = silu_parts(gate_pre)
    hidden = (activation * up_pre).astype(jnp.bfloat16)
    hidden_all = lax.all_gather(hidden, "fsdp", axis=3, tiled=True)
    expert_out = jnp.einsum(
        "jecf,efd->jecd", hidden_all, w_down, preferred_element_type=jnp.float32
    ).astype(jnp.bfloat16)
    shards = lax.axis_size("fsdp")
    exp_n, ff_all, feat = w_down.shape
    hidden_parts = jnp.einsum(
        "jecd,egfd->gjecf", cotangent, w_down.reshape(exp_n, shards, ff_all // shards, feat),
        preferred_element_type=jnp.float32,
    ).astype(jnp.bfloat16)
    grad_hidden = jnp.sum(
        lax.all_to_all(hidden_parts, "fsdp", 0, 0, tiled=False).astype(jnp.float32), axis=0
    )
    grad_gate_pre = (grad_hidden * up_pre * slope_term).astype(jnp.bfloat16)
    grad_up_pre = (grad_hidden * activation).astype(jnp.bfloat16)
    w_gate_g = w_gate.reshape(exp_n, w_gate.shape[1], shards, model_width // shards)
    w_up_g = w_up.reshape(exp_n, w_up.shape[1], shards, model_width // shards)
    input_parts = jnp.einsum(
        "jecf,efgd->gjecd", grad_gate_pre, w_gate_g, preferred_element_type=jnp.float32
    ) + jnp.einsum("jecf,efgd->gjecd", grad_up_pre, w_up_g, preferred_element_type=jnp.float32)
    input_slices = jnp.sum(
        lax.all_to_all(input_parts.astype(jnp.bfloat16), "fsdp", 0, 0, tiled=False).astype(
            jnp.float32
        ),
        axis=0,
    ).astype(jnp.bfloat16)
    feat = input_slices.shape[-1]
    both_back = lax.all_to_all(
        jnp.concatenate(
            [expert_out.reshape(slot_count, -1), input_slices.reshape(slot_count, -1)], axis=1
        ),
        "expert", split_axis=0, concat_axis=0, tiled=True,
    )
    mixed_slots, input_slots = both_back[:, :feat], both_back[:, feat:]
    mixed = jnp.dot(
        weighted.T, mixed_slots.astype(jnp.float32), precision=lax.Precision.HIGHEST
    ).astype(jnp.bfloat16)
    grad_tokens = jnp.dot(
        picker.T, input_slots.astype(jnp.float32), precision=lax.Precision.HIGHEST
    ).astype(jnp.bfloat16)
    grad_gate_w = rounded(
        jnp.einsum("jecf,jecd->efd", grad_gate_pre, received, preferred_element_type=jnp.float32)
    )
    grad_up_w = rounded(
        jnp.einsum("jecf,jecd->efd", grad_up_pre, received, preferred_element_type=jnp.float32)
    )
    grad_down_w = rounded(
        jnp.einsum("jecf,jecd->efd", hidden_all, cotangent, preferred_element_type=jnp.float32)
    )
    summed_gate = dp_reduce(grad_gate_w.astype(jnp.bfloat16), 2).astype(jnp.float32)
    summed_up = dp_reduce(grad_up_w.astype(jnp.bfloat16), 2).astype(jnp.float32)
    summed_down = dp_reduce(grad_down_w.astype(jnp.bfloat16), 1)
    return (
        mixed,
        grad_tokens,
        summed_gate.astype(jnp.bfloat16),
        summed_up.astype(jnp.bfloat16),
        summed_down,
    )


def solution(mesh):
    in_specs = (
        P(("dp", "expert"), "fsdp"),
        P(("dp", "expert"), "fsdp"),
        P(("dp", "expert"), None),
        P(("dp", "expert"), None),
        P("expert", "fsdp", None),
        P("expert", "fsdp", None),
        P("expert", None, "fsdp"),
    )
    out_specs = (
        P(("dp", "expert"), "fsdp"),
        P(("dp", "expert"), "fsdp"),
        P("expert", "fsdp", "dp"),
        P("expert", "fsdp", "dp"),
        P("expert", "dp", "fsdp"),
    )
    return jax.shard_map(body, mesh=mesh, in_specs=in_specs, out_specs=out_specs, check_vma=False)
```

```python
import jax
import jax.numpy as jnp
from jax import lax
from jax.sharding import PartitionSpec as P


def rounded(values):
    return lax.optimization_barrier(values.astype(jnp.bfloat16)).astype(jnp.float32)


def silu_parts(pre_act):
    sigmoid_value = jax.nn.sigmoid(pre_act)
    return (pre_act * sigmoid_value, sigmoid_value * (1.0 + pre_act * (1.0 - sigmoid_value)))


def dp_reduce(part, axis):
    groups = lax.axis_size("dp")
    if groups != 2:
        return lax.psum_scatter(part, "dp", scatter_dimension=axis, tiled=True)
    me = lax.axis_index("dp")
    halves = jnp.stack(jnp.split(part, 2, axis=axis))
    keep = lax.dynamic_index_in_dim(halves, me, 0, keepdims=False)
    send = lax.dynamic_index_in_dim(halves, 1 - me, 0, keepdims=False)
    got = lax.ppermute(send, "dp", perm=[(0, 1), (1, 0)])
    return (keep.astype(jnp.float32) + got.astype(jnp.float32)).astype(jnp.bfloat16)


def body(tokens, grad_out, expert_ids, gate_weights, w_gate, w_up, w_down):
    tok_rows = tokens.shape[0]
    choose = expert_ids.shape[1]
    exp_local = w_gate.shape[0]
    model_width = w_gate.shape[2]
    owners = lax.axis_size("expert")
    experts_all = owners * exp_local
    capacity = max(2, min(tok_rows, 5 * choose * tok_rows // (4 * experts_all)))
    slot_count = experts_all * capacity
    flat_ids = expert_ids.reshape(-1)
    onehot = (flat_ids[:, None] == jnp.arange(experts_all, dtype=jnp.int32)[None, :]).astype(
        jnp.int32
    )
    before = jnp.cumsum(onehot, axis=0) - onehot
    slot_rank = jnp.sum(before * onehot, axis=1)
    slot_of = (flat_ids * capacity + slot_rank).reshape(tok_rows, choose)
    placed = (slot_of[:, :, None] == jnp.arange(slot_count, dtype=jnp.int32)[None, None, :]).astype(
        jnp.float32
    )
    picker = jnp.sum(placed, axis=1).T
    weighted = jnp.einsum("tks,tk->st", placed, gate_weights, precision=lax.Precision.HIGHEST)
    picker_half = picker.astype(jnp.bfloat16)
    scaled_grad = jnp.dot(
        weighted, grad_out.astype(jnp.float32), precision=lax.Precision.HIGHEST
    ).astype(jnp.bfloat16)
    full_rows = lax.all_gather(tokens, "fsdp", axis=1, tiled=True)
    outgoing = jnp.dot(picker_half, full_rows, preferred_element_type=jnp.float32).astype(
        jnp.bfloat16
    )
    grads_in = lax.all_to_all(scaled_grad, "expert", split_axis=0, concat_axis=0, tiled=True)
    rows_in = lax.all_to_all(outgoing, "expert", split_axis=0, concat_axis=0, tiled=True)
    received = rows_in.reshape(owners, exp_local, capacity, model_width)
    cotangent = grads_in.reshape(owners, exp_local, capacity, -1)
    gate_pre = jnp.einsum("jecd,efd->jecf", received, w_gate, preferred_element_type=jnp.float32)
    up_pre = jnp.einsum("jecd,efd->jecf", received, w_up, preferred_element_type=jnp.float32)
    activation, slope_term = silu_parts(gate_pre)
    hidden = (activation * up_pre).astype(jnp.bfloat16)
    hidden_all = lax.all_gather(hidden, "fsdp", axis=3, tiled=True)
    expert_out = jnp.einsum(
        "jecf,efd->jecd", hidden_all, w_down, preferred_element_type=jnp.float32
    ).astype(jnp.bfloat16)
    shards = lax.axis_size("fsdp")
    exp_n, ff_all, feat = w_down.shape
    hidden_parts = jnp.einsum(
        "jecd,egfd->gjecf", cotangent, w_down.reshape(exp_n, shards, ff_all // shards, feat),
        preferred_element_type=jnp.float32,
    ).astype(jnp.bfloat16)
    grad_hidden = jnp.sum(
        lax.all_to_all(hidden_parts, "fsdp", 0, 0, tiled=False).astype(jnp.float32), axis=0
    )
    grad_gate_pre = (grad_hidden * up_pre * slope_term).astype(jnp.bfloat16)
    grad_up_pre = (grad_hidden * activation).astype(jnp.bfloat16)
    w_gate_g = w_gate.reshape(exp_n, w_gate.shape[1], shards, model_width // shards)
    w_up_g = w_up.reshape(exp_n, w_up.shape[1], shards, model_width // shards)
    input_parts = jnp.einsum(
        "jecf,efgd->gjecd", grad_gate_pre, w_gate_g, preferred_element_type=jnp.float32
    ) + jnp.einsum("jecf,efgd->gjecd", grad_up_pre, w_up_g, preferred_element_type=jnp.float32)
    input_slices = jnp.sum(
        lax.all_to_all(input_parts.astype(jnp.bfloat16), "fsdp", 0, 0, tiled=False).astype(
            jnp.float32
        ),
        axis=0,
    ).astype(jnp.bfloat16)
    mixed_slots = lax.all_to_all(
        expert_out.reshape(slot_count, -1), "expert", split_axis=0, concat_axis=0, tiled=True
    )
    input_slots = lax.all_to_all(
        input_slices.reshape(slot_count, -1), "expert", split_axis=0, concat_axis=0, tiled=True
    )
    mixed = jnp.dot(
        weighted.T, mixed_slots.astype(jnp.float32), precision=lax.Precision.HIGHEST
    ).astype(jnp.bfloat16)
    grad_tokens = jnp.dot(
        picker.T, input_slots.astype(jnp.float32), precision=lax.Precision.HIGHEST
    ).astype(jnp.bfloat16)
    grad_gate_w = rounded(
        jnp.einsum("jecf,jecd->efd", grad_gate_pre, received, preferred_element_type=jnp.float32)
    )
    grad_up_w = rounded(
        jnp.einsum("jecf,jecd->efd", grad_up_pre, received, preferred_element_type=jnp.float32)
    )
    grad_down_w = rounded(
        jnp.einsum("jecf,jecd->efd", hidden_all, cotangent, preferred_element_type=jnp.float32)
    )
    summed_gate = dp_reduce(grad_gate_w.astype(jnp.bfloat16), 2).astype(jnp.float32)
    summed_up = dp_reduce(grad_up_w.astype(jnp.bfloat16), 2).astype(jnp.float32)
    summed_down = dp_reduce(grad_down_w.astype(jnp.bfloat16), 1)
    return (
        mixed,
        grad_tokens,
        summed_gate.astype(jnp.bfloat16),
        summed_up.astype(jnp.bfloat16),
        summed_down,
    )


def solution(mesh):
    in_specs = (
        P(("dp", "expert"), "fsdp"),
        P(("dp", "expert"), "fsdp"),
        P(("dp", "expert"), None),
        P(("dp", "expert"), None),
        P("expert", "fsdp", None),
        P("expert", "fsdp", None),
        P("expert", None, "fsdp"),
    )
    out_specs = (
        P(("dp", "expert"), "fsdp"),
        P(("dp", "expert"), "fsdp"),
        P("expert", "fsdp", "dp"),
        P("expert", "fsdp", "dp"),
        P("expert", "dp", "fsdp"),
    )
    return jax.shard_map(body, mesh=mesh, in_specs=in_specs, out_specs=out_specs, check_vma=False)
```

```python
import jax
import jax.numpy as jnp
from jax import lax
from jax.sharding import PartitionSpec as P


def rounded(values):
    return lax.optimization_barrier(values.astype(jnp.bfloat16)).astype(jnp.float32)


def silu_parts(pre_act):
    sigmoid_value = jax.nn.sigmoid(pre_act)
    return (pre_act * sigmoid_value, sigmoid_value * (1.0 + pre_act * (1.0 - sigmoid_value)))


def dp_reduce(part, axis):
    groups = lax.axis_size("dp")
    if groups != 2:
        return lax.psum_scatter(part, "dp", scatter_dimension=axis, tiled=True)
    me = lax.axis_index("dp")
    halves = jnp.stack(jnp.split(part, 2, axis=axis))
    keep = lax.dynamic_index_in_dim(halves, me, 0, keepdims=False)
    send = lax.dynamic_index_in_dim(halves, 1 - me, 0, keepdims=False)
    got = lax.ppermute(send, "dp", perm=[(0, 1), (1, 0)])
    return (keep.astype(jnp.float32) + got.astype(jnp.float32)).astype(jnp.bfloat16)


def body(tokens, grad_out, expert_ids, gate_weights, w_gate, w_up, w_down):
    tok_rows = tokens.shape[0]
    choose = expert_ids.shape[1]
    exp_local = w_gate.shape[0]
    model_width = w_gate.shape[2]
    owners = lax.axis_size("expert")
    experts_all = owners * exp_local
    capacity = max(2, min(tok_rows, 5 * choose * tok_rows // (4 * experts_all)))
    slot_count = experts_all * capacity
    flat_ids = expert_ids.reshape(-1)
    onehot = (flat_ids[:, None] == jnp.arange(experts_all, dtype=jnp.int32)[None, :]).astype(
        jnp.int32
    )
    before = jnp.cumsum(onehot, axis=0) - onehot
    slot_rank = jnp.sum(before * onehot, axis=1)
    slot_of = (flat_ids * capacity + slot_rank).reshape(tok_rows, choose)
    placed = (slot_of[:, :, None] == jnp.arange(slot_count, dtype=jnp.int32)[None, None, :]).astype(
        jnp.float32
    )
    picker = jnp.sum(placed, axis=1).T
    weighted = jnp.einsum("tks,tk->st", placed, gate_weights, precision=lax.Precision.HIGHEST)
    picker_half = picker.astype(jnp.bfloat16)
    scaled_grad = jnp.dot(
        weighted, grad_out.astype(jnp.float32), precision=lax.Precision.HIGHEST
    ).astype(jnp.bfloat16)
    outgoing = jnp.dot(picker_half, tokens, preferred_element_type=jnp.float32).astype(
        jnp.bfloat16
    )
    local_feat = tokens.shape[1]
    both_in = lax.all_to_all(
        jnp.concatenate([outgoing, scaled_grad], axis=1),
        "expert", split_axis=0, concat_axis=0, tiled=True,
    )
    rows_in = lax.all_gather(both_in[:, :local_feat], "fsdp", axis=1, tiled=True)
    grads_in = both_in[:, local_feat:]
    received = rows_in.reshape(owners, exp_local, capacity, model_width)
    cotangent = grads_in.reshape(owners, exp_local, capacity, -1)
    gate_pre = jnp.einsum("jecd,efd->jecf", received, w_gate, preferred_element_type=jnp.float32)
    up_pre = jnp.einsum("jecd,efd->jecf", received, w_up, preferred_element_type=jnp.float32)
    activation, slope_term = silu_parts(gate_pre)
    hidden = (activation * up_pre).astype(jnp.bfloat16)
    hidden_all = lax.all_gather(hidden, "fsdp", axis=3, tiled=True)
    expert_out = jnp.einsum(
        "jecf,efd->jecd", hidden_all, w_down, preferred_element_type=jnp.float32
    ).astype(jnp.bfloat16)
    shards = lax.axis_size("fsdp")
    exp_n, ff_all, feat = w_down.shape
    hidden_parts = jnp.einsum(
        "jecd,egfd->gjecf", cotangent, w_down.reshape(exp_n, shards, ff_all // shards, feat),
        preferred_element_type=jnp.float32,
    ).astype(jnp.bfloat16)
    grad_hidden = jnp.sum(
        lax.all_to_all(hidden_parts, "fsdp", 0, 0, tiled=False).astype(jnp.float32), axis=0
    )
    grad_gate_pre = (grad_hidden * up_pre * slope_term).astype(jnp.bfloat16)
    grad_up_pre = (grad_hidden * activation).astype(jnp.bfloat16)
    w_gate_g = w_gate.reshape(exp_n, w_gate.shape[1], shards, model_width // shards)
    w_up_g = w_up.reshape(exp_n, w_up.shape[1], shards, model_width // shards)
    input_parts = jnp.einsum(
        "jecf,efgd->gjecd", grad_gate_pre, w_gate_g, preferred_element_type=jnp.float32
    ) + jnp.einsum("jecf,efgd->gjecd", grad_up_pre, w_up_g, preferred_element_type=jnp.float32)
    input_slices = jnp.sum(
        lax.all_to_all(input_parts.astype(jnp.bfloat16), "fsdp", 0, 0, tiled=False).astype(
            jnp.float32
        ),
        axis=0,
    ).astype(jnp.bfloat16)
    feat = input_slices.shape[-1]
    both_back = lax.all_to_all(
        jnp.concatenate(
            [expert_out.reshape(slot_count, -1), input_slices.reshape(slot_count, -1)], axis=1
        ),
        "expert", split_axis=0, concat_axis=0, tiled=True,
    )
    mixed_slots, input_slots = both_back[:, :feat], both_back[:, feat:]
    mixed = jnp.dot(
        weighted.T, mixed_slots.astype(jnp.float32), precision=lax.Precision.HIGHEST
    ).astype(jnp.bfloat16)
    grad_tokens = jnp.dot(
        picker.T, input_slots.astype(jnp.float32), precision=lax.Precision.HIGHEST
    ).astype(jnp.bfloat16)
    grad_gate_w = rounded(
        jnp.einsum("jecf,jecd->efd", grad_gate_pre, received, preferred_element_type=jnp.float32)
    )
    grad_up_w = rounded(
        jnp.einsum("jecf,jecd->efd", grad_up_pre, received, preferred_element_type=jnp.float32)
    )
    grad_down_w = rounded(
        jnp.einsum("jecf,jecd->efd", hidden_all, cotangent, preferred_element_type=jnp.float32)
    )
    summed_gate = dp_reduce(grad_gate_w.astype(jnp.bfloat16), 2).astype(jnp.float32)
    summed_up = dp_reduce(grad_up_w.astype(jnp.bfloat16), 2).astype(jnp.float32)
    summed_down = dp_reduce(grad_down_w.astype(jnp.bfloat16), 1)
    return (
        mixed,
        grad_tokens,
        summed_gate.astype(jnp.bfloat16),
        summed_up.astype(jnp.bfloat16),
        summed_down,
    )


def solution(mesh):
    in_specs = (
        P(("dp", "expert"), "fsdp"),
        P(("dp", "expert"), "fsdp"),
        P(("dp", "expert"), None),
        P(("dp", "expert"), None),
        P("expert", "fsdp", None),
        P("expert", "fsdp", None),
        P("expert", None, "fsdp"),
    )
    out_specs = (
        P(("dp", "expert"), "fsdp"),
        P(("dp", "expert"), "fsdp"),
        P("expert", "fsdp", "dp"),
        P("expert", "fsdp", "dp"),
        P("expert", "dp", "fsdp"),
    )
    return jax.shard_map(body, mesh=mesh, in_specs=in_specs, out_specs=out_specs, check_vma=False)
```

```python
import jax
import jax.numpy as jnp
from jax import lax
from jax.sharding import PartitionSpec as P


def rounded(values):
    return lax.optimization_barrier(values.astype(jnp.bfloat16)).astype(jnp.float32)


def silu_parts(pre_act):
    sigmoid_value = jax.nn.sigmoid(pre_act)
    return (pre_act * sigmoid_value, sigmoid_value * (1.0 + pre_act * (1.0 - sigmoid_value)))


def dp_reduce(part, axis):
    groups = lax.axis_size("dp")
    if groups != 2:
        return lax.psum_scatter(part, "dp", scatter_dimension=axis, tiled=True)
    me = lax.axis_index("dp")
    halves = jnp.stack(jnp.split(part, 2, axis=axis))
    keep = lax.dynamic_index_in_dim(halves, me, 0, keepdims=False)
    send = lax.dynamic_index_in_dim(halves, 1 - me, 0, keepdims=False)
    got = lax.ppermute(send, "dp", perm=[(0, 1), (1, 0)])
    return (keep.astype(jnp.float32) + got.astype(jnp.float32)).astype(jnp.bfloat16)


def gather_fsdp(part, axis):
    over_z = lax.all_gather(part, "fz", axis=axis, tiled=False)
    both = lax.all_gather(over_z, "fc", axis=axis, tiled=False)
    both = jnp.swapaxes(both, axis, axis + 1)
    shape = part.shape[:axis] + (-1,) + part.shape[axis + 1:]
    return both.reshape(shape)


def reduce_fsdp(parts):
    n_z, n_c = lax.axis_size("fz"), lax.axis_size("fc")
    split = parts.reshape((n_z, n_c) + parts.shape[1:])
    on_chip = lax.all_to_all(split, "fc", 1, 1, tiled=False)
    paired = jnp.sum(on_chip.astype(jnp.float32), axis=1).astype(jnp.bfloat16)
    return jnp.sum(lax.all_to_all(paired, "fz", 0, 0, tiled=False).astype(jnp.float32), axis=0)


def body(tokens, grad_out, expert_ids, gate_weights, w_gate, w_up, w_down):
    tok_rows = tokens.shape[0]
    choose = expert_ids.shape[1]
    exp_local = w_gate.shape[0]
    model_width = w_gate.shape[2]
    owners = lax.axis_size("expert")
    experts_all = owners * exp_local
    capacity = max(2, min(tok_rows, 5 * choose * tok_rows // (4 * experts_all)))
    slot_count = experts_all * capacity
    flat_ids = expert_ids.reshape(-1)
    onehot = (flat_ids[:, None] == jnp.arange(experts_all, dtype=jnp.int32)[None, :]).astype(
        jnp.int32
    )
    before = jnp.cumsum(onehot, axis=0) - onehot
    slot_rank = jnp.sum(before * onehot, axis=1)
    slot_of = (flat_ids * capacity + slot_rank).reshape(tok_rows, choose)
    placed = (slot_of[:, :, None] == jnp.arange(slot_count, dtype=jnp.int32)[None, None, :]).astype(
        jnp.float32
    )
    picker = jnp.sum(placed, axis=1).T
    weighted = jnp.einsum("tks,tk->st", placed, gate_weights, precision=lax.Precision.HIGHEST)
    picker_half = picker.astype(jnp.bfloat16)
    scaled_grad = jnp.dot(
        weighted, grad_out.astype(jnp.float32), precision=lax.Precision.HIGHEST
    ).astype(jnp.bfloat16)
    outgoing = jnp.dot(picker_half, tokens, preferred_element_type=jnp.float32).astype(
        jnp.bfloat16
    )
    local_feat = tokens.shape[1]
    both_in = lax.all_to_all(
        jnp.concatenate([outgoing, scaled_grad], axis=1),
        "expert", split_axis=0, concat_axis=0, tiled=True,
    )
    rows_in = gather_fsdp(both_in[:, :local_feat], 1)
    grads_in = both_in[:, local_feat:]
    received = rows_in.reshape(owners, exp_local, capacity, model_width)
    cotangent = grads_in.reshape(owners, exp_local, capacity, -1)
    gate_pre = jnp.einsum("jecd,efd->jecf", received, w_gate, preferred_element_type=jnp.float32)
    up_pre = jnp.einsum("jecd,efd->jecf", received, w_up, preferred_element_type=jnp.float32)
    activation, slope_term = silu_parts(gate_pre)
    hidden = (activation * up_pre).astype(jnp.bfloat16)
    hidden_all = gather_fsdp(hidden, 3)
    expert_out = jnp.einsum(
        "jecf,efd->jecd", hidden_all, w_down, preferred_element_type=jnp.float32
    ).astype(jnp.bfloat16)
    shards = lax.axis_size("fz") * lax.axis_size("fc")
    exp_n, ff_all, feat = w_down.shape
    hidden_parts = jnp.einsum(
        "jecd,egfd->gjecf", cotangent, w_down.reshape(exp_n, shards, ff_all // shards, feat),
        preferred_element_type=jnp.float32,
    ).astype(jnp.bfloat16)
    grad_hidden = reduce_fsdp(hidden_parts)
    grad_gate_pre = (grad_hidden * up_pre * slope_term).astype(jnp.bfloat16)
    grad_up_pre = (grad_hidden * activation).astype(jnp.bfloat16)
    w_gate_g = w_gate.reshape(exp_n, w_gate.shape[1], shards, model_width // shards)
    w_up_g = w_up.reshape(exp_n, w_up.shape[1], shards, model_width // shards)
    input_parts = jnp.einsum(
        "jecf,efgd->gjecd", grad_gate_pre, w_gate_g, preferred_element_type=jnp.float32
    ) + jnp.einsum("jecf,efgd->gjecd", grad_up_pre, w_up_g, preferred_element_type=jnp.float32)
    input_slices = reduce_fsdp(input_parts.astype(jnp.bfloat16)).astype(jnp.bfloat16)
    feat = input_slices.shape[-1]
    both_back = lax.all_to_all(
        jnp.concatenate(
            [expert_out.reshape(slot_count, -1), input_slices.reshape(slot_count, -1)], axis=1
        ),
        "expert", split_axis=0, concat_axis=0, tiled=True,
    )
    mixed_slots, input_slots = both_back[:, :feat], both_back[:, feat:]
    mixed = jnp.dot(
        weighted.T, mixed_slots.astype(jnp.float32), precision=lax.Precision.HIGHEST
    ).astype(jnp.bfloat16)
    grad_tokens = jnp.dot(
        picker.T, input_slots.astype(jnp.float32), precision=lax.Precision.HIGHEST
    ).astype(jnp.bfloat16)
    grad_gate_w = rounded(
        jnp.einsum("jecf,jecd->efd", grad_gate_pre, received, preferred_element_type=jnp.float32)
    )
    grad_up_w = rounded(
        jnp.einsum("jecf,jecd->efd", grad_up_pre, received, preferred_element_type=jnp.float32)
    )
    grad_down_w = rounded(
        jnp.einsum("jecf,jecd->efd", hidden_all, cotangent, preferred_element_type=jnp.float32)
    )
    summed_gate = dp_reduce(grad_gate_w.astype(jnp.bfloat16), 2).astype(jnp.float32)
    summed_up = dp_reduce(grad_up_w.astype(jnp.bfloat16), 2).astype(jnp.float32)
    summed_down = dp_reduce(grad_down_w.astype(jnp.bfloat16), 1)
    return (
        mixed,
        grad_tokens,
        summed_gate.astype(jnp.bfloat16),
        summed_up.astype(jnp.bfloat16),
        summed_down,
    )


def solution(mesh):
    in_specs = (
        P(("dp", "expert"), ("fz", "fc")),
        P(("dp", "expert"), ("fz", "fc")),
        P(("dp", "expert"), None),
        P(("dp", "expert"), None),
        P("expert", ("fz", "fc"), None),
        P("expert", ("fz", "fc"), None),
        P("expert", None, ("fz", "fc")),
    )
    out_specs = (
        P(("dp", "expert"), ("fz", "fc")),
        P(("dp", "expert"), ("fz", "fc")),
        P("expert", ("fz", "fc"), "dp"),
        P("expert", ("fz", "fc"), "dp"),
        P("expert", "dp", ("fz", "fc")),
    )
    n_fsdp = mesh.shape["fsdp"]
    split_mesh = jax.sharding.Mesh(
        mesh.devices.reshape(mesh.devices.shape[:-1] + (n_fsdp // 2, 2)),
        mesh.axis_names[:-1] + ("fz", "fc"),
    )
    return jax.shard_map(body, mesh=split_mesh, in_specs=in_specs, out_specs=out_specs, check_vma=False)
```

```python
import jax
import jax.numpy as jnp
from jax import lax
from jax.sharding import PartitionSpec as P


def rounded(values):
    return lax.optimization_barrier(values.astype(jnp.bfloat16)).astype(jnp.float32)


def silu_parts(pre_act):
    sigmoid_value = jax.nn.sigmoid(pre_act)
    return (pre_act * sigmoid_value, sigmoid_value * (1.0 + pre_act * (1.0 - sigmoid_value)))


def dp_reduce(part, axis):
    groups = lax.axis_size("dp")
    if groups != 2:
        return lax.psum_scatter(part, "dp", scatter_dimension=axis, tiled=True)
    me = lax.axis_index("dp")
    halves = jnp.stack(jnp.split(part, 2, axis=axis))
    keep = lax.dynamic_index_in_dim(halves, me, 0, keepdims=False)
    send = lax.dynamic_index_in_dim(halves, 1 - me, 0, keepdims=False)
    got = lax.ppermute(send, "dp", perm=[(0, 1), (1, 0)])
    return (keep.astype(jnp.float32) + got.astype(jnp.float32)).astype(jnp.bfloat16)


def gather_fsdp(part, axis):
    shards = lax.axis_size("fsdp")
    copies = jnp.broadcast_to(part[None], (shards,) + part.shape)
    got = lax.all_to_all(copies, "fsdp", 0, 0, tiled=False)
    got = jnp.moveaxis(got, 0, axis)
    return got.reshape(part.shape[:axis] + (-1,) + part.shape[axis + 1:])


def body(tokens, grad_out, expert_ids, gate_weights, w_gate, w_up, w_down):
    tok_rows = tokens.shape[0]
    choose = expert_ids.shape[1]
    exp_local = w_gate.shape[0]
    model_width = w_gate.shape[2]
    owners = lax.axis_size("expert")
    experts_all = owners * exp_local
    capacity = max(2, min(tok_rows, 5 * choose * tok_rows // (4 * experts_all)))
    slot_count = experts_all * capacity
    flat_ids = expert_ids.reshape(-1)
    onehot = (flat_ids[:, None] == jnp.arange(experts_all, dtype=jnp.int32)[None, :]).astype(
        jnp.int32
    )
    before = jnp.cumsum(onehot, axis=0) - onehot
    slot_rank = jnp.sum(before * onehot, axis=1)
    slot_of = (flat_ids * capacity + slot_rank).reshape(tok_rows, choose)
    placed = (slot_of[:, :, None] == jnp.arange(slot_count, dtype=jnp.int32)[None, None, :]).astype(
        jnp.float32
    )
    picker = jnp.sum(placed, axis=1).T
    weighted = jnp.einsum("tks,tk->st", placed, gate_weights, precision=lax.Precision.HIGHEST)
    picker_half = picker.astype(jnp.bfloat16)
    scaled_grad = jnp.dot(
        weighted, grad_out.astype(jnp.float32), precision=lax.Precision.HIGHEST
    ).astype(jnp.bfloat16)
    outgoing = jnp.dot(picker_half, tokens, preferred_element_type=jnp.float32).astype(
        jnp.bfloat16
    )
    local_feat = tokens.shape[1]
    both_in = lax.all_to_all(
        jnp.concatenate([outgoing, scaled_grad], axis=1),
        "expert", split_axis=0, concat_axis=0, tiled=True,
    )
    rows_in = gather_fsdp(both_in[:, :local_feat], 1)
    grads_in = both_in[:, local_feat:]
    received = rows_in.reshape(owners, exp_local, capacity, model_width)
    cotangent = grads_in.reshape(owners, exp_local, capacity, -1)
    gate_pre = jnp.einsum("jecd,efd->jecf", received, w_gate, preferred_element_type=jnp.float32)
    up_pre = jnp.einsum("jecd,efd->jecf", received, w_up, preferred_element_type=jnp.float32)
    activation, slope_term = silu_parts(gate_pre)
    hidden = (activation * up_pre).astype(jnp.bfloat16)
    hidden_all = gather_fsdp(hidden, 3)
    expert_out = jnp.einsum(
        "jecf,efd->jecd", hidden_all, w_down, preferred_element_type=jnp.float32
    ).astype(jnp.bfloat16)
    shards = lax.axis_size("fsdp")
    exp_n, ff_all, feat = w_down.shape
    hidden_parts = jnp.einsum(
        "jecd,egfd->gjecf", cotangent, w_down.reshape(exp_n, shards, ff_all // shards, feat),
        preferred_element_type=jnp.float32,
    ).astype(jnp.bfloat16)
    grad_hidden = jnp.sum(
        lax.all_to_all(hidden_parts, "fsdp", 0, 0, tiled=False).astype(jnp.float32), axis=0
    )
    grad_gate_pre = (grad_hidden * up_pre * slope_term).astype(jnp.bfloat16)
    grad_up_pre = (grad_hidden * activation).astype(jnp.bfloat16)
    w_gate_g = w_gate.reshape(exp_n, w_gate.shape[1], shards, model_width // shards)
    w_up_g = w_up.reshape(exp_n, w_up.shape[1], shards, model_width // shards)
    input_parts = jnp.einsum(
        "jecf,efgd->gjecd", grad_gate_pre, w_gate_g, preferred_element_type=jnp.float32
    ) + jnp.einsum("jecf,efgd->gjecd", grad_up_pre, w_up_g, preferred_element_type=jnp.float32)
    input_slices = jnp.sum(
        lax.all_to_all(input_parts.astype(jnp.bfloat16), "fsdp", 0, 0, tiled=False).astype(
            jnp.float32
        ),
        axis=0,
    ).astype(jnp.bfloat16)
    feat = input_slices.shape[-1]
    both_back = lax.all_to_all(
        jnp.concatenate(
            [expert_out.reshape(slot_count, -1), input_slices.reshape(slot_count, -1)], axis=1
        ),
        "expert", split_axis=0, concat_axis=0, tiled=True,
    )
    mixed_slots, input_slots = both_back[:, :feat], both_back[:, feat:]
    mixed = jnp.dot(
        weighted.T, mixed_slots.astype(jnp.float32), precision=lax.Precision.HIGHEST
    ).astype(jnp.bfloat16)
    grad_tokens = jnp.dot(
        picker.T, input_slots.astype(jnp.float32), precision=lax.Precision.HIGHEST
    ).astype(jnp.bfloat16)
    grad_gate_w = rounded(
        jnp.einsum("jecf,jecd->efd", grad_gate_pre, received, preferred_element_type=jnp.float32)
    )
    grad_up_w = rounded(
        jnp.einsum("jecf,jecd->efd", grad_up_pre, received, preferred_element_type=jnp.float32)
    )
    grad_down_w = rounded(
        jnp.einsum("jecf,jecd->efd", hidden_all, cotangent, preferred_element_type=jnp.float32)
    )
    summed_gate = dp_reduce(grad_gate_w.astype(jnp.bfloat16), 2).astype(jnp.float32)
    summed_up = dp_reduce(grad_up_w.astype(jnp.bfloat16), 2).astype(jnp.float32)
    summed_down = dp_reduce(grad_down_w.astype(jnp.bfloat16), 1)
    return (
        mixed,
        grad_tokens,
        summed_gate.astype(jnp.bfloat16),
        summed_up.astype(jnp.bfloat16),
        summed_down,
    )


def solution(mesh):
    in_specs = (
        P(("dp", "expert"), "fsdp"),
        P(("dp", "expert"), "fsdp"),
        P(("dp", "expert"), None),
        P(("dp", "expert"), None),
        P("expert", "fsdp", None),
        P("expert", "fsdp", None),
        P("expert", None, "fsdp"),
    )
    out_specs = (
        P(("dp", "expert"), "fsdp"),
        P(("dp", "expert"), "fsdp"),
        P("expert", "fsdp", "dp"),
        P("expert", "fsdp", "dp"),
        P("expert", "dp", "fsdp"),
    )
    return jax.shard_map(body, mesh=mesh, in_specs=in_specs, out_specs=out_specs, check_vma=False)
```

```python
import jax
import jax.numpy as jnp
from jax import lax
from jax.sharding import PartitionSpec as P


def rounded(values):
    return lax.optimization_barrier(values.astype(jnp.bfloat16)).astype(jnp.float32)


def silu_parts(pre_act):
    sigmoid_value = jax.nn.sigmoid(pre_act)
    return (pre_act * sigmoid_value, sigmoid_value * (1.0 + pre_act * (1.0 - sigmoid_value)))


def dp_reduce(part, axis):
    groups = lax.axis_size("dp")
    if groups != 2:
        return lax.psum_scatter(part, "dp", scatter_dimension=axis, tiled=True)
    me = lax.axis_index("dp")
    halves = jnp.stack(jnp.split(part, 2, axis=axis))
    keep = lax.dynamic_index_in_dim(halves, me, 0, keepdims=False)
    send = lax.dynamic_index_in_dim(halves, 1 - me, 0, keepdims=False)
    got = lax.ppermute(send, "dp", perm=[(0, 1), (1, 0)])
    return (keep.astype(jnp.float32) + got.astype(jnp.float32)).astype(jnp.bfloat16)


def gather_fsdp(part, axis):
    shards = lax.axis_size("fsdp")
    copies = jnp.broadcast_to(part[None], (shards,) + part.shape)
    got = lax.all_to_all(copies, "fsdp", 0, 0, tiled=False)
    got = jnp.moveaxis(got, 0, axis)
    return got.reshape(part.shape[:axis] + (-1,) + part.shape[axis + 1:])


def body(tokens, grad_out, expert_ids, gate_weights, w_gate, w_up, w_down):
    tok_rows = tokens.shape[0]
    choose = expert_ids.shape[1]
    exp_local = w_gate.shape[0]
    model_width = w_gate.shape[2]
    owners = lax.axis_size("expert")
    experts_all = owners * exp_local
    capacity = max(2, min(tok_rows, 5 * choose * tok_rows // (4 * experts_all)))
    slot_count = experts_all * capacity
    flat_ids = expert_ids.reshape(-1)
    onehot = (flat_ids[:, None] == jnp.arange(experts_all, dtype=jnp.int32)[None, :]).astype(
        jnp.int32
    )
    before = jnp.cumsum(onehot, axis=0) - onehot
    slot_rank = jnp.sum(before * onehot, axis=1)
    slot_of = (flat_ids * capacity + slot_rank).reshape(tok_rows, choose)
    placed = (slot_of[:, :, None] == jnp.arange(slot_count, dtype=jnp.int32)[None, None, :]).astype(
        jnp.float32
    )
    picker = jnp.sum(placed, axis=1).T
    weighted = jnp.einsum("tks,tk->st", placed, gate_weights, precision=lax.Precision.HIGHEST)
    picker_half = picker.astype(jnp.bfloat16)
    scaled_grad = jnp.dot(
        weighted, grad_out.astype(jnp.float32), precision=lax.Precision.HIGHEST
    ).astype(jnp.bfloat16)
    outgoing = jnp.dot(picker_half, tokens, preferred_element_type=jnp.float32).astype(
        jnp.bfloat16
    )
    local_feat = tokens.shape[1]
    both_in = lax.all_to_all(
        jnp.concatenate([outgoing, scaled_grad], axis=1),
        "expert", split_axis=0, concat_axis=0, tiled=True,
    )
    rows_in = gather_fsdp(both_in[:, :local_feat], 1)
    grads_in = both_in[:, local_feat:]
    received = rows_in.reshape(owners, exp_local, capacity, model_width)
    cotangent = grads_in.reshape(owners, exp_local, capacity, -1)
    gate_pre = jnp.einsum("jecd,efd->jecf", received, w_gate, preferred_element_type=jnp.float32)
    up_pre = jnp.einsum("jecd,efd->jecf", received, w_up, preferred_element_type=jnp.float32)
    activation, slope_term = silu_parts(gate_pre)
    hidden = (activation * up_pre).astype(jnp.bfloat16)
    hidden_all = gather_fsdp(hidden, 3)
    expert_out = jnp.einsum(
        "jecf,efd->jecd", hidden_all, w_down, preferred_element_type=jnp.float32
    ).astype(jnp.bfloat16)
    shards = lax.axis_size("fsdp")
    exp_n, ff_all, feat = w_down.shape
    hidden_parts = jnp.einsum(
        "jecd,egfd->gjecf", cotangent, w_down.reshape(exp_n, shards, ff_all // shards, feat),
        preferred_element_type=jnp.float32,
    ).astype(jnp.bfloat16)
    grad_hidden = jnp.sum(
        lax.all_to_all(hidden_parts, "fsdp", 0, 0, tiled=False).astype(jnp.float32), axis=0
    )
    grad_gate_pre = (grad_hidden * up_pre * slope_term).astype(jnp.bfloat16)
    grad_up_pre = (grad_hidden * activation).astype(jnp.bfloat16)
    w_gate_g = w_gate.reshape(exp_n, w_gate.shape[1], shards, model_width // shards)
    w_up_g = w_up.reshape(exp_n, w_up.shape[1], shards, model_width // shards)
    input_parts = jnp.einsum(
        "jecf,efgd->gjecd", grad_gate_pre, w_gate_g, preferred_element_type=jnp.float32
    ) + jnp.einsum("jecf,efgd->gjecd", grad_up_pre, w_up_g, preferred_element_type=jnp.float32)
    input_slices = jnp.sum(
        lax.all_to_all(input_parts.astype(jnp.bfloat16), "fsdp", 0, 0, tiled=False).astype(
            jnp.float32
        ),
        axis=0,
    ).astype(jnp.bfloat16)
    feat = input_slices.shape[-1]
    both_back = lax.all_to_all(
        jnp.concatenate(
            [expert_out.reshape(slot_count, -1), input_slices.reshape(slot_count, -1)], axis=1
        ),
        "expert", split_axis=0, concat_axis=0, tiled=True,
    )
    mixed_slots, input_slots = both_back[:, :feat], both_back[:, feat:]
    mixed = jnp.dot(
        weighted.T, mixed_slots.astype(jnp.float32), precision=lax.Precision.HIGHEST
    ).astype(jnp.bfloat16)
    grad_tokens = jnp.dot(
        picker.T, input_slots.astype(jnp.float32), precision=lax.Precision.HIGHEST
    ).astype(jnp.bfloat16)
    me = lax.axis_index("dp")
    half_feat = model_width // 2
    half_ff = hidden_all.shape[3] // 2

    def half(values, which):
        size = values.shape[3] // 2
        return lax.dynamic_slice_in_dim(values, which * size, size, axis=3)

    first = lax.ppermute(
        jnp.concatenate([half(received, 1 - me), cotangent], axis=3), "dp", perm=[(0, 1), (1, 0)]
    )
    rows_other, cot_other = first[..., :half_feat], first[..., half_feat:]
    second = lax.ppermute(
        jnp.concatenate([grad_gate_pre, grad_up_pre, half(hidden_all, 1 - me)], axis=3),
        "dp", perm=[(0, 1), (1, 0)],
    )
    ff_local = grad_gate_pre.shape[3]
    gate_other = second[..., :ff_local]
    up_other = second[..., ff_local:2 * ff_local]
    hidden_other = second[..., 2 * ff_local:]
    rows_mine = half(received, me)

    def group_sum(left, right):
        return rounded(jnp.einsum("jecf,jecd->efd", left, right, preferred_element_type=jnp.float32))

    summed_gate = group_sum(grad_gate_pre, rows_mine) + group_sum(gate_other, rows_other)
    summed_up = group_sum(grad_up_pre, rows_mine) + group_sum(up_other, rows_other)
    summed_down = (
        group_sum(half(hidden_all, me), cotangent) + group_sum(hidden_other, cot_other)
    ).astype(jnp.bfloat16)
    return (
        mixed,
        grad_tokens,
        summed_gate.astype(jnp.bfloat16),
        summed_up.astype(jnp.bfloat16),
        summed_down,
    )


def solution(mesh):
    in_specs = (
        P(("dp", "expert"), "fsdp"),
        P(("dp", "expert"), "fsdp"),
        P(("dp", "expert"), None),
        P(("dp", "expert"), None),
        P("expert", "fsdp", None),
        P("expert", "fsdp", None),
        P("expert", None, "fsdp"),
    )
    out_specs = (
        P(("dp", "expert"), "fsdp"),
        P(("dp", "expert"), "fsdp"),
        P("expert", "fsdp", "dp"),
        P("expert", "fsdp", "dp"),
        P("expert", "dp", "fsdp"),
    )
    return jax.shard_map(body, mesh=mesh, in_specs=in_specs, out_specs=out_specs, check_vma=False)
```

```python
import jax
import jax.numpy as jnp
from jax import lax
from jax.sharding import PartitionSpec as P


def rounded(values):
    return lax.optimization_barrier(values.astype(jnp.bfloat16)).astype(jnp.float32)


def silu_parts(pre_act):
    sigmoid_value = jax.nn.sigmoid(pre_act)
    return (pre_act * sigmoid_value, sigmoid_value * (1.0 + pre_act * (1.0 - sigmoid_value)))


def dp_reduce(part, axis):
    groups = lax.axis_size("dp")
    if groups != 2:
        return lax.psum_scatter(part, "dp", scatter_dimension=axis, tiled=True)
    me = lax.axis_index("dp")
    halves = jnp.stack(jnp.split(part, 2, axis=axis))
    keep = lax.dynamic_index_in_dim(halves, me, 0, keepdims=False)
    send = lax.dynamic_index_in_dim(halves, 1 - me, 0, keepdims=False)
    got = lax.ppermute(send, "dp", perm=[(0, 1), (1, 0)])
    return (keep.astype(jnp.float32) + got.astype(jnp.float32)).astype(jnp.bfloat16)


def gather_fsdp(part, axis):
    shards = lax.axis_size("fsdp")
    copies = jnp.broadcast_to(part[None], (shards,) + part.shape)
    got = lax.all_to_all(copies, "fsdp", 0, 0, tiled=False)
    got = jnp.moveaxis(got, 0, axis)
    return got.reshape(part.shape[:axis] + (-1,) + part.shape[axis + 1:])


def body(tokens, grad_out, expert_ids, gate_weights, w_gate, w_up, w_down):
    tok_rows = tokens.shape[0]
    choose = expert_ids.shape[1]
    exp_local = w_gate.shape[0]
    model_width = w_gate.shape[2]
    owners = lax.axis_size("expert")
    experts_all = owners * exp_local
    capacity = max(2, min(tok_rows, 5 * choose * tok_rows // (4 * experts_all)))
    slot_count = experts_all * capacity
    flat_ids = expert_ids.reshape(-1)
    onehot = (flat_ids[:, None] == jnp.arange(experts_all, dtype=jnp.int32)[None, :]).astype(
        jnp.int32
    )
    before = jnp.cumsum(onehot, axis=0) - onehot
    slot_rank = jnp.sum(before * onehot, axis=1)
    slot_of = (flat_ids * capacity + slot_rank).reshape(tok_rows, choose)
    placed = (slot_of[:, :, None] == jnp.arange(slot_count, dtype=jnp.int32)[None, None, :]).astype(
        jnp.float32
    )
    picker = jnp.sum(placed, axis=1).T
    weighted = jnp.einsum("tks,tk->st", placed, gate_weights, precision=lax.Precision.HIGHEST)
    picker_half = picker.astype(jnp.bfloat16)
    scaled_grad = jnp.dot(
        weighted, grad_out.astype(jnp.float32), precision=lax.Precision.HIGHEST
    ).astype(jnp.bfloat16)
    outgoing = jnp.dot(picker_half, tokens, preferred_element_type=jnp.float32).astype(
        jnp.bfloat16
    )
    local_feat = tokens.shape[1]
    both_in = lax.all_to_all(
        jnp.concatenate([outgoing, scaled_grad], axis=1),
        "expert", split_axis=0, concat_axis=0, tiled=True,
    )
    grads_in = both_in[:, local_feat:]
    cotangent = grads_in.reshape(owners, exp_local, capacity, -1)
    shards = lax.axis_size("fsdp")
    exp_n, ff_all, feat = w_down.shape
    ff_local = ff_all // shards
    hidden_parts = jnp.einsum(
        "jecd,egfd->gjecf", cotangent, w_down.reshape(exp_n, shards, ff_local, feat),
        preferred_element_type=jnp.float32,
    ).astype(jnp.bfloat16)
    rows_part = both_in[:, :local_feat]
    first = lax.all_to_all(
        jnp.concatenate(
            [
                jnp.broadcast_to(rows_part[None], (shards,) + rows_part.shape),
                hidden_parts.reshape(shards, slot_count, ff_local),
            ],
            axis=2,
        ),
        "fsdp", 0, 0, tiled=False,
    )
    rows_in = jnp.moveaxis(first[..., :local_feat], 0, 1).reshape(slot_count, model_width)
    grad_hidden = jnp.sum(first[..., local_feat:].astype(jnp.float32), axis=0).reshape(
        owners, exp_local, capacity, ff_local
    )
    received = rows_in.reshape(owners, exp_local, capacity, model_width)
    gate_pre = jnp.einsum("jecd,efd->jecf", received, w_gate, preferred_element_type=jnp.float32)
    up_pre = jnp.einsum("jecd,efd->jecf", received, w_up, preferred_element_type=jnp.float32)
    activation, slope_term = silu_parts(gate_pre)
    hidden = (activation * up_pre).astype(jnp.bfloat16)
    grad_gate_pre = (grad_hidden * up_pre * slope_term).astype(jnp.bfloat16)
    grad_up_pre = (grad_hidden * activation).astype(jnp.bfloat16)
    w_gate_g = w_gate.reshape(exp_n, w_gate.shape[1], shards, model_width // shards)
    w_up_g = w_up.reshape(exp_n, w_up.shape[1], shards, model_width // shards)
    input_parts = jnp.einsum(
        "jecf,efgd->gjecd", grad_gate_pre, w_gate_g, preferred_element_type=jnp.float32
    ) + jnp.einsum("jecf,efgd->gjecd", grad_up_pre, w_up_g, preferred_element_type=jnp.float32)
    hidden_flat = hidden.reshape(slot_count, ff_local)
    second = lax.all_to_all(
        jnp.concatenate(
            [
                jnp.broadcast_to(hidden_flat[None], (shards,) + hidden_flat.shape),
                input_parts.astype(jnp.bfloat16).reshape(shards, slot_count, feat),
            ],
            axis=2,
        ),
        "fsdp", 0, 0, tiled=False,
    )
    hidden_all = jnp.moveaxis(second[..., :ff_local], 0, 1).reshape(
        owners, exp_local, capacity, ff_all
    )
    input_slices = jnp.sum(second[..., ff_local:].astype(jnp.float32), axis=0).astype(jnp.bfloat16)
    expert_out = jnp.einsum(
        "jecf,efd->jecd", hidden_all, w_down, preferred_element_type=jnp.float32
    ).astype(jnp.bfloat16)
    feat = input_slices.shape[-1]
    both_back = lax.all_to_all(
        jnp.concatenate(
            [expert_out.reshape(slot_count, -1), input_slices.reshape(slot_count, -1)], axis=1
        ),
        "expert", split_axis=0, concat_axis=0, tiled=True,
    )
    mixed_slots, input_slots = both_back[:, :feat], both_back[:, feat:]
    mixed = jnp.dot(
        weighted.T, mixed_slots.astype(jnp.float32), precision=lax.Precision.HIGHEST
    ).astype(jnp.bfloat16)
    grad_tokens = jnp.dot(
        picker.T, input_slots.astype(jnp.float32), precision=lax.Precision.HIGHEST
    ).astype(jnp.bfloat16)
    grad_gate_w = rounded(
        jnp.einsum("jecf,jecd->efd", grad_gate_pre, received, preferred_element_type=jnp.float32)
    )
    grad_up_w = rounded(
        jnp.einsum("jecf,jecd->efd", grad_up_pre, received, preferred_element_type=jnp.float32)
    )
    grad_down_w = rounded(
        jnp.einsum("jecf,jecd->efd", hidden_all, cotangent, preferred_element_type=jnp.float32)
    )
    summed_gate = dp_reduce(grad_gate_w.astype(jnp.bfloat16), 2).astype(jnp.float32)
    summed_up = dp_reduce(grad_up_w.astype(jnp.bfloat16), 2).astype(jnp.float32)
    summed_down = dp_reduce(grad_down_w.astype(jnp.bfloat16), 1)
    return (
        mixed,
        grad_tokens,
        summed_gate.astype(jnp.bfloat16),
        summed_up.astype(jnp.bfloat16),
        summed_down,
    )


def solution(mesh):
    in_specs = (
        P(("dp", "expert"), "fsdp"),
        P(("dp", "expert"), "fsdp"),
        P(("dp", "expert"), None),
        P(("dp", "expert"), None),
        P("expert", "fsdp", None),
        P("expert", "fsdp", None),
        P("expert", None, "fsdp"),
    )
    out_specs = (
        P(("dp", "expert"), "fsdp"),
        P(("dp", "expert"), "fsdp"),
        P("expert", "fsdp", "dp"),
        P("expert", "fsdp", "dp"),
        P("expert", "dp", "fsdp"),
    )
    return jax.shard_map(body, mesh=mesh, in_specs=in_specs, out_specs=out_specs, check_vma=False)
```

```python
import jax
import jax.numpy as jnp
from jax import lax
from jax.sharding import PartitionSpec as P


def rounded(values):
    return lax.optimization_barrier(values.astype(jnp.bfloat16)).astype(jnp.float32)


def silu_parts(pre_act):
    sigmoid_value = jax.nn.sigmoid(pre_act)
    return (pre_act * sigmoid_value, sigmoid_value * (1.0 + pre_act * (1.0 - sigmoid_value)))


def dp_reduce(part, axis):
    groups = lax.axis_size("dp")
    if groups != 2:
        return lax.psum_scatter(part, "dp", scatter_dimension=axis, tiled=True)
    me = lax.axis_index("dp")
    halves = jnp.stack(jnp.split(part, 2, axis=axis))
    keep = lax.dynamic_index_in_dim(halves, me, 0, keepdims=False)
    send = lax.dynamic_index_in_dim(halves, 1 - me, 0, keepdims=False)
    got = lax.ppermute(send, "dp", perm=[(0, 1), (1, 0)])
    return (keep.astype(jnp.float32) + got.astype(jnp.float32)).astype(jnp.bfloat16)


def gather_fsdp(part, axis):
    shards = lax.axis_size("fsdp")
    copies = jnp.broadcast_to(part[None], (shards,) + part.shape)
    got = lax.all_to_all(copies, "fsdp", 0, 0, tiled=False)
    got = jnp.moveaxis(got, 0, axis)
    return got.reshape(part.shape[:axis] + (-1,) + part.shape[axis + 1:])


def body(tokens, grad_out, expert_ids, gate_weights, w_gate, w_up, w_down):
    tok_rows = tokens.shape[0]
    choose = expert_ids.shape[1]
    exp_local = w_gate.shape[0]
    model_width = w_gate.shape[2]
    owners = lax.axis_size("expert")
    experts_all = owners * exp_local
    capacity = max(2, min(tok_rows, 5 * choose * tok_rows // (4 * experts_all)))
    slot_count = experts_all * capacity
    flat_ids = expert_ids.reshape(-1)
    onehot = (flat_ids[:, None] == jnp.arange(experts_all, dtype=jnp.int32)[None, :]).astype(
        jnp.int32
    )
    before = jnp.cumsum(onehot, axis=0) - onehot
    slot_rank = jnp.sum(before * onehot, axis=1)
    slot_of = (flat_ids * capacity + slot_rank).reshape(tok_rows, choose)
    placed = (slot_of[:, :, None] == jnp.arange(slot_count, dtype=jnp.int32)[None, None, :]).astype(
        jnp.float32
    )
    picker = jnp.sum(placed, axis=1).T
    weighted = jnp.einsum("tks,tk->st", placed, gate_weights, precision=lax.Precision.HIGHEST)
    picker_half = picker.astype(jnp.bfloat16)
    scaled_grad = jnp.dot(
        weighted, grad_out.astype(jnp.float32), precision=lax.Precision.HIGHEST
    ).astype(jnp.bfloat16)
    outgoing = jnp.dot(picker_half, tokens, preferred_element_type=jnp.float32).astype(
        jnp.bfloat16
    )
    local_feat = tokens.shape[1]
    both_in = lax.all_to_all(
        jnp.concatenate([outgoing, scaled_grad], axis=1),
        "expert", split_axis=0, concat_axis=0, tiled=True,
    )
    rows_in = gather_fsdp(both_in[:, :local_feat], 1)
    grads_in = both_in[:, local_feat:]
    received = rows_in.reshape(owners, exp_local, capacity, model_width)
    cotangent = grads_in.reshape(owners, exp_local, capacity, -1)
    gate_pre = jnp.einsum("jecd,efd->jecf", received, w_gate, preferred_element_type=jnp.float32)
    up_pre = jnp.einsum("jecd,efd->jecf", received, w_up, preferred_element_type=jnp.float32)
    activation, slope_term = silu_parts(gate_pre)
    hidden = (activation * up_pre).astype(jnp.bfloat16)
    hidden_all = gather_fsdp(hidden, 3)
    expert_out = jnp.einsum(
        "jecf,efd->jecd", hidden_all, w_down, preferred_element_type=jnp.float32
    ).astype(jnp.bfloat16)
    shards = lax.axis_size("fsdp")
    exp_n, ff_all, feat = w_down.shape
    hidden_parts = jnp.einsum(
        "jecd,egfd->gjecf", cotangent, w_down.reshape(exp_n, shards, ff_all // shards, feat),
        preferred_element_type=jnp.float32,
    ).astype(jnp.bfloat16)
    grad_hidden = jnp.sum(
        lax.all_to_all(hidden_parts, "fsdp", 0, 0, tiled=False).astype(jnp.float32), axis=0
    )
    grad_gate_pre = (grad_hidden * up_pre * slope_term).astype(jnp.bfloat16)
    grad_up_pre = (grad_hidden * activation).astype(jnp.bfloat16)
    w_gate_g = w_gate.reshape(exp_n, w_gate.shape[1], shards, model_width // shards)
    w_up_g = w_up.reshape(exp_n, w_up.shape[1], shards, model_width // shards)
    input_parts = jnp.einsum(
        "jecf,efgd->gjecd", grad_gate_pre, w_gate_g, preferred_element_type=jnp.float32
    ) + jnp.einsum("jecf,efgd->gjecd", grad_up_pre, w_up_g, preferred_element_type=jnp.float32)
    input_slices = jnp.sum(
        lax.all_to_all(input_parts.astype(jnp.bfloat16), "fsdp", 0, 0, tiled=False).astype(
            jnp.float32
        ),
        axis=0,
    ).astype(jnp.bfloat16)
    feat = input_slices.shape[-1]
    both_back = lax.all_to_all(
        jnp.concatenate(
            [expert_out.reshape(slot_count, -1), input_slices.reshape(slot_count, -1)], axis=1
        ),
        "expert", split_axis=0, concat_axis=0, tiled=True,
    )
    mixed_slots, input_slots = both_back[:, :feat], both_back[:, feat:]
    mixed = jnp.dot(
        weighted.T, mixed_slots.astype(jnp.float32), precision=lax.Precision.HIGHEST
    ).astype(jnp.bfloat16)
    grad_tokens = jnp.dot(
        picker.T, input_slots.astype(jnp.float32), precision=lax.Precision.HIGHEST
    ).astype(jnp.bfloat16)
    grad_gate_w = rounded(
        jnp.einsum("jecf,jecd->efd", grad_gate_pre, received, preferred_element_type=jnp.float32)
    )
    grad_up_w = rounded(
        jnp.einsum("jecf,jecd->efd", grad_up_pre, received, preferred_element_type=jnp.float32)
    )
    grad_down_w = rounded(
        jnp.einsum("jecf,jecd->efd", hidden_all, cotangent, preferred_element_type=jnp.float32)
    )
    summed_gate, summed_up = dp_reduce(
        jnp.stack([grad_gate_w, grad_up_w]).astype(jnp.bfloat16), 3
    ).astype(jnp.float32)
    summed_down = dp_reduce(grad_down_w.astype(jnp.bfloat16), 1)
    return (
        mixed,
        grad_tokens,
        summed_gate.astype(jnp.bfloat16),
        summed_up.astype(jnp.bfloat16),
        summed_down,
    )


def solution(mesh):
    in_specs = (
        P(("dp", "expert"), "fsdp"),
        P(("dp", "expert"), "fsdp"),
        P(("dp", "expert"), None),
        P(("dp", "expert"), None),
        P("expert", "fsdp", None),
        P("expert", "fsdp", None),
        P("expert", None, "fsdp"),
    )
    out_specs = (
        P(("dp", "expert"), "fsdp"),
        P(("dp", "expert"), "fsdp"),
        P("expert", "fsdp", "dp"),
        P("expert", "fsdp", "dp"),
        P("expert", "dp", "fsdp"),
    )
    return jax.shard_map(body, mesh=mesh, in_specs=in_specs, out_specs=out_specs, check_vma=False)
```

```python
import jax
import jax.numpy as jnp
from jax import lax
from jax.sharding import PartitionSpec as P


def rounded(values):
    return lax.optimization_barrier(values.astype(jnp.bfloat16)).astype(jnp.float32)


def silu_parts(pre_act):
    sigmoid_value = jax.nn.sigmoid(pre_act)
    return (pre_act * sigmoid_value, sigmoid_value * (1.0 + pre_act * (1.0 - sigmoid_value)))


def dp_reduce(part, axis):
    groups = lax.axis_size("dp")
    if groups != 2:
        return lax.psum_scatter(part, "dp", scatter_dimension=axis, tiled=True)
    me = lax.axis_index("dp")
    halves = jnp.stack(jnp.split(part, 2, axis=axis))
    keep = lax.dynamic_index_in_dim(halves, me, 0, keepdims=False)
    send = lax.dynamic_index_in_dim(halves, 1 - me, 0, keepdims=False)
    got = lax.ppermute(send, "dp", perm=[(0, 1), (1, 0)])
    return (keep.astype(jnp.float32) + got.astype(jnp.float32)).astype(jnp.bfloat16)


def gather_fsdp(part, axis):
    shards = lax.axis_size("fsdp")
    copies = jnp.broadcast_to(part[None], (shards,) + part.shape)
    got = lax.all_to_all(copies, "fsdp", 0, 0, tiled=False)
    got = jnp.moveaxis(got, 0, axis)
    return got.reshape(part.shape[:axis] + (-1,) + part.shape[axis + 1:])


def body(tokens, grad_out, expert_ids, gate_weights, w_gate, w_up, w_down):
    tok_rows = tokens.shape[0]
    choose = expert_ids.shape[1]
    exp_local = w_gate.shape[0]
    model_width = w_gate.shape[2]
    owners = lax.axis_size("expert")
    experts_all = owners * exp_local
    capacity = max(2, min(tok_rows, 5 * choose * tok_rows // (4 * experts_all)))
    slot_count = experts_all * capacity
    flat_ids = expert_ids.reshape(-1)
    onehot = (flat_ids[:, None] == jnp.arange(experts_all, dtype=jnp.int32)[None, :]).astype(
        jnp.int32
    )
    before = jnp.cumsum(onehot, axis=0) - onehot
    slot_rank = jnp.sum(before * onehot, axis=1)
    slot_of = (flat_ids * capacity + slot_rank).reshape(tok_rows, choose)
    placed = (slot_of[:, :, None] == jnp.arange(slot_count, dtype=jnp.int32)[None, None, :]).astype(
        jnp.float32
    )
    picker = jnp.sum(placed, axis=1).T
    weighted = jnp.einsum("tks,tk->st", placed, gate_weights, precision=lax.Precision.HIGHEST)
    picker_half = picker.astype(jnp.bfloat16)
    scaled_grad = jnp.dot(
        weighted, grad_out.astype(jnp.float32), precision=lax.Precision.HIGHEST
    ).astype(jnp.bfloat16)
    outgoing = jnp.dot(picker_half, tokens, preferred_element_type=jnp.float32).astype(
        jnp.bfloat16
    )
    local_feat = tokens.shape[1]
    both_in = lax.all_to_all(
        jnp.concatenate([outgoing, scaled_grad], axis=1),
        "expert", split_axis=0, concat_axis=0, tiled=True,
    )
    rows_in = gather_fsdp(both_in[:, :local_feat], 1)
    grads_in = both_in[:, local_feat:]
    received = rows_in.reshape(owners, exp_local, capacity, model_width)
    cotangent = grads_in.reshape(owners, exp_local, capacity, -1)
    gate_pre = jnp.einsum("jecd,efd->jecf", received, w_gate, preferred_element_type=jnp.float32)
    up_pre = jnp.einsum("jecd,efd->jecf", received, w_up, preferred_element_type=jnp.float32)
    activation, slope_term = silu_parts(gate_pre)
    hidden = (activation * up_pre).astype(jnp.bfloat16)
    hidden_all = gather_fsdp(hidden, 3)
    expert_out = jnp.einsum(
        "jecf,efd->jecd", hidden_all, w_down, preferred_element_type=jnp.float32
    ).astype(jnp.bfloat16)
    shards = lax.axis_size("fsdp")
    exp_n, ff_all, feat = w_down.shape
    hidden_parts = jnp.einsum(
        "jecd,egfd->gjecf", cotangent, w_down.reshape(exp_n, shards, ff_all // shards, feat),
        preferred_element_type=jnp.float32,
    ).astype(jnp.bfloat16)
    grad_hidden = jnp.sum(
        lax.all_to_all(hidden_parts, "fsdp", 0, 0, tiled=False).astype(jnp.float32), axis=0
    )
    grad_gate_pre = (grad_hidden * up_pre * slope_term).astype(jnp.bfloat16)
    grad_up_pre = (grad_hidden * activation).astype(jnp.bfloat16)
    w_gate_g = w_gate.reshape(exp_n, w_gate.shape[1], shards, model_width // shards)
    w_up_g = w_up.reshape(exp_n, w_up.shape[1], shards, model_width // shards)
    input_parts = jnp.einsum(
        "jecf,efgd->gjecd", grad_gate_pre, w_gate_g, preferred_element_type=jnp.float32
    ) + jnp.einsum("jecf,efgd->gjecd", grad_up_pre, w_up_g, preferred_element_type=jnp.float32)
    input_slices = jnp.sum(
        lax.all_to_all(input_parts.astype(jnp.bfloat16), "fsdp", 0, 0, tiled=False).astype(
            jnp.float32
        ),
        axis=0,
    ).astype(jnp.bfloat16)
    feat = input_slices.shape[-1]
    both_back = lax.all_to_all(
        jnp.concatenate(
            [expert_out.reshape(slot_count, -1), input_slices.reshape(slot_count, -1)], axis=1
        ),
        "expert", split_axis=0, concat_axis=0, tiled=True,
    )
    mixed_slots, input_slots = both_back[:, :feat], both_back[:, feat:]
    mixed = jnp.dot(
        weighted.T, mixed_slots.astype(jnp.float32), precision=lax.Precision.HIGHEST
    ).astype(jnp.bfloat16)
    grad_tokens = jnp.dot(
        picker.T, input_slots.astype(jnp.float32), precision=lax.Precision.HIGHEST
    ).astype(jnp.bfloat16)
    grad_gate_w = rounded(
        jnp.einsum("jecf,jecd->efd", grad_gate_pre, received, preferred_element_type=jnp.float32)
    )
    grad_up_w = rounded(
        jnp.einsum("jecf,jecd->efd", grad_up_pre, received, preferred_element_type=jnp.float32)
    )
    grad_down_w = rounded(
        jnp.einsum("jecf,jecd->efd", hidden_all, cotangent, preferred_element_type=jnp.float32)
    )
    summed_gate, summed_up = lax.psum_scatter(
        jnp.stack([grad_gate_w, grad_up_w]).astype(jnp.bfloat16), "dp", scatter_dimension=3,
        tiled=True,
    ).astype(jnp.float32)
    summed_down = dp_reduce(grad_down_w.astype(jnp.bfloat16), 1)
    return (
        mixed,
        grad_tokens,
        summed_gate.astype(jnp.bfloat16),
        summed_up.astype(jnp.bfloat16),
        summed_down,
    )


def solution(mesh):
    in_specs = (
        P(("dp", "expert"), "fsdp"),
        P(("dp", "expert"), "fsdp"),
        P(("dp", "expert"), None),
        P(("dp", "expert"), None),
        P("expert", "fsdp", None),
        P("expert", "fsdp", None),
        P("expert", None, "fsdp"),
    )
    out_specs = (
        P(("dp", "expert"), "fsdp"),
        P(("dp", "expert"), "fsdp"),
        P("expert", "fsdp", "dp"),
        P("expert", "fsdp", "dp"),
        P("expert", "dp", "fsdp"),
    )
    return jax.shard_map(body, mesh=mesh, in_specs=in_specs, out_specs=out_specs, check_vma=False)
```

```python
import jax
import jax.numpy as jnp
from jax import lax
from jax.sharding import PartitionSpec as P


def rounded(values):
    return lax.optimization_barrier(values.astype(jnp.bfloat16)).astype(jnp.float32)


def silu_parts(pre_act):
    sigmoid_value = jax.nn.sigmoid(pre_act)
    return (pre_act * sigmoid_value, sigmoid_value * (1.0 + pre_act * (1.0 - sigmoid_value)))


def dp_reduce(part, axis):
    groups = lax.axis_size("dp")
    if groups != 2:
        return lax.psum_scatter(part, "dp", scatter_dimension=axis, tiled=True)
    me = lax.axis_index("dp")
    halves = jnp.stack(jnp.split(part, 2, axis=axis))
    keep = lax.dynamic_index_in_dim(halves, me, 0, keepdims=False)
    send = lax.dynamic_index_in_dim(halves, 1 - me, 0, keepdims=False)
    got = lax.ppermute(send, "dp", perm=[(0, 1), (1, 0)])
    return (keep.astype(jnp.float32) + got.astype(jnp.float32)).astype(jnp.bfloat16)


def gather_fsdp(part, axis):
    shards = lax.axis_size("fsdp")
    copies = jnp.broadcast_to(part[None], (shards,) + part.shape)
    got = lax.all_to_all(copies, "fsdp", 0, 0, tiled=False)
    got = jnp.moveaxis(got, 0, axis)
    return got.reshape(part.shape[:axis] + (-1,) + part.shape[axis + 1:])


def body(tokens, grad_out, expert_ids, gate_weights, w_gate, w_up, w_down):
    tok_rows = tokens.shape[0]
    choose = expert_ids.shape[1]
    exp_local = w_gate.shape[0]
    model_width = w_gate.shape[2]
    owners = lax.axis_size("expert")
    experts_all = owners * exp_local
    capacity = max(2, min(tok_rows, 5 * choose * tok_rows // (4 * experts_all)))
    slot_count = experts_all * capacity
    flat_ids = expert_ids.reshape(-1)
    onehot = (flat_ids[:, None] == jnp.arange(experts_all, dtype=jnp.int32)[None, :]).astype(
        jnp.int32
    )
    before = jnp.cumsum(onehot, axis=0) - onehot
    slot_rank = jnp.sum(before * onehot, axis=1)
    slot_of = (flat_ids * capacity + slot_rank).reshape(tok_rows, choose)
    placed = (slot_of[:, :, None] == jnp.arange(slot_count, dtype=jnp.int32)[None, None, :]).astype(
        jnp.float32
    )
    picker = jnp.sum(placed, axis=1).T
    weighted = jnp.einsum("tks,tk->st", placed, gate_weights, precision=lax.Precision.HIGHEST)
    picker_half = picker.astype(jnp.bfloat16)
    scaled_grad = jnp.dot(
        weighted, grad_out.astype(jnp.float32), precision=lax.Precision.HIGHEST
    ).astype(jnp.bfloat16)
    outgoing = jnp.dot(picker_half, tokens, preferred_element_type=jnp.float32).astype(
        jnp.bfloat16
    )
    local_feat = tokens.shape[1]
    both_in = lax.all_to_all(
        jnp.concatenate([outgoing, scaled_grad], axis=1),
        "expert", split_axis=0, concat_axis=0, tiled=True,
    )
    rows_in = lax.all_gather(both_in[:, :local_feat], "fsdp", axis=1, tiled=True)
    grads_in = both_in[:, local_feat:]
    received = rows_in.reshape(owners, exp_local, capacity, model_width)
    cotangent = grads_in.reshape(owners, exp_local, capacity, -1)
    gate_pre = jnp.einsum("jecd,efd->jecf", received, w_gate, preferred_element_type=jnp.float32)
    up_pre = jnp.einsum("jecd,efd->jecf", received, w_up, preferred_element_type=jnp.float32)
    activation, slope_term = silu_parts(gate_pre)
    hidden = (activation * up_pre).astype(jnp.bfloat16)
    hidden_all = gather_fsdp(hidden, 3)
    expert_out = jnp.einsum(
        "jecf,efd->jecd", hidden_all, w_down, preferred_element_type=jnp.float32
    ).astype(jnp.bfloat16)
    shards = lax.axis_size("fsdp")
    exp_n, ff_all, feat = w_down.shape
    hidden_parts = jnp.einsum(
        "jecd,egfd->gjecf", cotangent, w_down.reshape(exp_n, shards, ff_all // shards, feat),
        preferred_element_type=jnp.float32,
    ).astype(jnp.bfloat16)
    grad_hidden = jnp.sum(
        lax.all_to_all(hidden_parts, "fsdp", 0, 0, tiled=False).astype(jnp.float32), axis=0
    )
    grad_gate_pre = (grad_hidden * up_pre * slope_term).astype(jnp.bfloat16)
    grad_up_pre = (grad_hidden * activation).astype(jnp.bfloat16)
    w_gate_g = w_gate.reshape(exp_n, w_gate.shape[1], shards, model_width // shards)
    w_up_g = w_up.reshape(exp_n, w_up.shape[1], shards, model_width // shards)
    input_parts = jnp.einsum(
        "jecf,efgd->gjecd", grad_gate_pre, w_gate_g, preferred_element_type=jnp.float32
    ) + jnp.einsum("jecf,efgd->gjecd", grad_up_pre, w_up_g, preferred_element_type=jnp.float32)
    input_slices = jnp.sum(
        lax.all_to_all(input_parts.astype(jnp.bfloat16), "fsdp", 0, 0, tiled=False).astype(
            jnp.float32
        ),
        axis=0,
    ).astype(jnp.bfloat16)
    feat = input_slices.shape[-1]
    both_back = lax.all_to_all(
        jnp.concatenate(
            [expert_out.reshape(slot_count, -1), input_slices.reshape(slot_count, -1)], axis=1
        ),
        "expert", split_axis=0, concat_axis=0, tiled=True,
    )
    mixed_slots, input_slots = both_back[:, :feat], both_back[:, feat:]
    mixed = jnp.dot(
        weighted.T, mixed_slots.astype(jnp.float32), precision=lax.Precision.HIGHEST
    ).astype(jnp.bfloat16)
    grad_tokens = jnp.dot(
        picker.T, input_slots.astype(jnp.float32), precision=lax.Precision.HIGHEST
    ).astype(jnp.bfloat16)
    grad_gate_w = rounded(
        jnp.einsum("jecf,jecd->efd", grad_gate_pre, received, preferred_element_type=jnp.float32)
    )
    grad_up_w = rounded(
        jnp.einsum("jecf,jecd->efd", grad_up_pre, received, preferred_element_type=jnp.float32)
    )
    grad_down_w = rounded(
        jnp.einsum("jecf,jecd->efd", hidden_all, cotangent, preferred_element_type=jnp.float32)
    )
    summed_gate, summed_up = dp_reduce(
        jnp.stack([grad_gate_w, grad_up_w]).astype(jnp.bfloat16), 3
    ).astype(jnp.float32)
    summed_down = dp_reduce(grad_down_w.astype(jnp.bfloat16), 1)
    return (
        mixed,
        grad_tokens,
        summed_gate.astype(jnp.bfloat16),
        summed_up.astype(jnp.bfloat16),
        summed_down,
    )


def solution(mesh):
    in_specs = (
        P(("dp", "expert"), "fsdp"),
        P(("dp", "expert"), "fsdp"),
        P(("dp", "expert"), None),
        P(("dp", "expert"), None),
        P("expert", "fsdp", None),
        P("expert", "fsdp", None),
        P("expert", None, "fsdp"),
    )
    out_specs = (
        P(("dp", "expert"), "fsdp"),
        P(("dp", "expert"), "fsdp"),
        P("expert", "fsdp", "dp"),
        P("expert", "fsdp", "dp"),
        P("expert", "dp", "fsdp"),
    )
    return jax.shard_map(body, mesh=mesh, in_specs=in_specs, out_specs=out_specs, check_vma=False)
```

```python
import jax
import jax.numpy as jnp
from jax import lax
from jax.sharding import PartitionSpec as P


def rounded(values):
    return lax.optimization_barrier(values.astype(jnp.bfloat16)).astype(jnp.float32)


def silu_parts(pre_act):
    sigmoid_value = jax.nn.sigmoid(pre_act)
    return (pre_act * sigmoid_value, sigmoid_value * (1.0 + pre_act * (1.0 - sigmoid_value)))


def dp_reduce(part, axis):
    groups = lax.axis_size("dp")
    if groups != 2:
        return lax.psum_scatter(part, "dp", scatter_dimension=axis, tiled=True)
    me = lax.axis_index("dp")
    halves = jnp.stack(jnp.split(part, 2, axis=axis))
    keep = lax.dynamic_index_in_dim(halves, me, 0, keepdims=False)
    send = lax.dynamic_index_in_dim(halves, 1 - me, 0, keepdims=False)
    got = lax.ppermute(send, "dp", perm=[(0, 1), (1, 0)])
    return (keep.astype(jnp.float32) + got.astype(jnp.float32)).astype(jnp.bfloat16)


def gather_fsdp(part, axis):
    shards = lax.axis_size("fsdp")
    copies = jnp.broadcast_to(part[None], (shards,) + part.shape)
    got = lax.all_to_all(copies, "fsdp", 0, 0, tiled=False)
    got = jnp.moveaxis(got, 0, axis)
    return got.reshape(part.shape[:axis] + (-1,) + part.shape[axis + 1:])


def dp_reduce_many(parts, axes):
    me = lax.axis_index("dp")
    keeps, sends = [], []
    for part, axis in zip(parts, axes):
        halves = jnp.stack(jnp.split(part, 2, axis=axis))
        keeps.append(lax.dynamic_index_in_dim(halves, me, 0, keepdims=False))
        sends.append(lax.dynamic_index_in_dim(halves, 1 - me, 0, keepdims=False))
    got = lax.ppermute(
        jnp.concatenate([x.reshape(-1) for x in sends]), "dp", perm=[(0, 1), (1, 0)]
    )
    outs, at = [], 0
    for keep in keeps:
        piece = got[at:at + keep.size].reshape(keep.shape)
        at += keep.size
        outs.append((keep.astype(jnp.float32) + piece.astype(jnp.float32)).astype(jnp.bfloat16))
    return outs[0][0], outs[0][1], outs[1]


def body(tokens, grad_out, expert_ids, gate_weights, w_gate, w_up, w_down):
    tok_rows = tokens.shape[0]
    choose = expert_ids.shape[1]
    exp_local = w_gate.shape[0]
    model_width = w_gate.shape[2]
    owners = lax.axis_size("expert")
    experts_all = owners * exp_local
    capacity = max(2, min(tok_rows, 5 * choose * tok_rows // (4 * experts_all)))
    slot_count = experts_all * capacity
    flat_ids = expert_ids.reshape(-1)
    onehot = (flat_ids[:, None] == jnp.arange(experts_all, dtype=jnp.int32)[None, :]).astype(
        jnp.int32
    )
    before = jnp.cumsum(onehot, axis=0) - onehot
    slot_rank = jnp.sum(before * onehot, axis=1)
    slot_of = (flat_ids * capacity + slot_rank).reshape(tok_rows, choose)
    placed = (slot_of[:, :, None] == jnp.arange(slot_count, dtype=jnp.int32)[None, None, :]).astype(
        jnp.float32
    )
    picker = jnp.sum(placed, axis=1).T
    weighted = jnp.einsum("tks,tk->st", placed, gate_weights, precision=lax.Precision.HIGHEST)
    picker_half = picker.astype(jnp.bfloat16)
    scaled_grad = jnp.dot(
        weighted, grad_out.astype(jnp.float32), precision=lax.Precision.HIGHEST
    ).astype(jnp.bfloat16)
    outgoing = jnp.dot(picker_half, tokens, preferred_element_type=jnp.float32).astype(
        jnp.bfloat16
    )
    local_feat = tokens.shape[1]
    both_in = lax.all_to_all(
        jnp.concatenate([outgoing, scaled_grad], axis=1),
        "expert", split_axis=0, concat_axis=0, tiled=True,
    )
    rows_in = lax.all_gather(both_in[:, :local_feat], "fsdp", axis=1, tiled=True)
    grads_in = both_in[:, local_feat:]
    received = rows_in.reshape(owners, exp_local, capacity, model_width)
    cotangent = grads_in.reshape(owners, exp_local, capacity, -1)
    gate_pre = jnp.einsum("jecd,efd->jecf", received, w_gate, preferred_element_type=jnp.float32)
    up_pre = jnp.einsum("jecd,efd->jecf", received, w_up, preferred_element_type=jnp.float32)
    activation, slope_term = silu_parts(gate_pre)
    hidden = (activation * up_pre).astype(jnp.bfloat16)
    hidden_all = gather_fsdp(hidden, 3)
    expert_out = jnp.einsum(
        "jecf,efd->jecd", hidden_all, w_down, preferred_element_type=jnp.float32
    ).astype(jnp.bfloat16)
    shards = lax.axis_size("fsdp")
    exp_n, ff_all, feat = w_down.shape
    hidden_parts = jnp.einsum(
        "jecd,egfd->gjecf", cotangent, w_down.reshape(exp_n, shards, ff_all // shards, feat),
        preferred_element_type=jnp.float32,
    ).astype(jnp.bfloat16)
    grad_hidden = jnp.sum(
        lax.all_to_all(hidden_parts, "fsdp", 0, 0, tiled=False).astype(jnp.float32), axis=0
    )
    grad_gate_pre = (grad_hidden * up_pre * slope_term).astype(jnp.bfloat16)
    grad_up_pre = (grad_hidden * activation).astype(jnp.bfloat16)
    w_gate_g = w_gate.reshape(exp_n, w_gate.shape[1], shards, model_width // shards)
    w_up_g = w_up.reshape(exp_n, w_up.shape[1], shards, model_width // shards)
    input_parts = jnp.einsum(
        "jecf,efgd->gjecd", grad_gate_pre, w_gate_g, preferred_element_type=jnp.float32
    ) + jnp.einsum("jecf,efgd->gjecd", grad_up_pre, w_up_g, preferred_element_type=jnp.float32)
    input_slices = jnp.sum(
        lax.all_to_all(input_parts.astype(jnp.bfloat16), "fsdp", 0, 0, tiled=False).astype(
            jnp.float32
        ),
        axis=0,
    ).astype(jnp.bfloat16)
    feat = input_slices.shape[-1]
    both_back = lax.all_to_all(
        jnp.concatenate(
            [expert_out.reshape(slot_count, -1), input_slices.reshape(slot_count, -1)], axis=1
        ),
        "expert", split_axis=0, concat_axis=0, tiled=True,
    )
    mixed_slots, input_slots = both_back[:, :feat], both_back[:, feat:]
    mixed = jnp.dot(
        weighted.T, mixed_slots.astype(jnp.float32), precision=lax.Precision.HIGHEST
    ).astype(jnp.bfloat16)
    grad_tokens = jnp.dot(
        picker.T, input_slots.astype(jnp.float32), precision=lax.Precision.HIGHEST
    ).astype(jnp.bfloat16)
    grad_gate_w = rounded(
        jnp.einsum("jecf,jecd->efd", grad_gate_pre, received, preferred_element_type=jnp.float32)
    )
    grad_up_w = rounded(
        jnp.einsum("jecf,jecd->efd", grad_up_pre, received, preferred_element_type=jnp.float32)
    )
    grad_down_w = rounded(
        jnp.einsum("jecf,jecd->efd", hidden_all, cotangent, preferred_element_type=jnp.float32)
    )
    summed_gate, summed_up, summed_down = dp_reduce_many(
        [jnp.stack([grad_gate_w, grad_up_w]).astype(jnp.bfloat16), grad_down_w.astype(jnp.bfloat16)],
        [3, 1],
    )
    summed_gate = summed_gate.astype(jnp.float32)
    summed_up = summed_up.astype(jnp.float32)
    return (
        mixed,
        grad_tokens,
        summed_gate.astype(jnp.bfloat16),
        summed_up.astype(jnp.bfloat16),
        summed_down,
    )


def solution(mesh):
    in_specs = (
        P(("dp", "expert"), "fsdp"),
        P(("dp", "expert"), "fsdp"),
        P(("dp", "expert"), None),
        P(("dp", "expert"), None),
        P("expert", "fsdp", None),
        P("expert", "fsdp", None),
        P("expert", None, "fsdp"),
    )
    out_specs = (
        P(("dp", "expert"), "fsdp"),
        P(("dp", "expert"), "fsdp"),
        P("expert", "fsdp", "dp"),
        P("expert", "fsdp", "dp"),
        P("expert", "dp", "fsdp"),
    )
    return jax.shard_map(body, mesh=mesh, in_specs=in_specs, out_specs=out_specs, check_vma=False)
```

```python
import jax
import jax.numpy as jnp
from jax import lax
from jax.sharding import PartitionSpec as P


def rounded(values):
    return lax.optimization_barrier(values.astype(jnp.bfloat16)).astype(jnp.float32)


def silu_parts(pre_act):
    sigmoid_value = jax.nn.sigmoid(pre_act)
    return (pre_act * sigmoid_value, sigmoid_value * (1.0 + pre_act * (1.0 - sigmoid_value)))


def dp_reduce(part, axis):
    groups = lax.axis_size("dp")
    if groups != 2:
        return lax.psum_scatter(part, "dp", scatter_dimension=axis, tiled=True)
    me = lax.axis_index("dp")
    halves = jnp.stack(jnp.split(part, 2, axis=axis))
    keep = lax.dynamic_index_in_dim(halves, me, 0, keepdims=False)
    send = lax.dynamic_index_in_dim(halves, 1 - me, 0, keepdims=False)
    got = lax.ppermute(send, "dp", perm=[(0, 1), (1, 0)])
    return (keep.astype(jnp.float32) + got.astype(jnp.float32)).astype(jnp.bfloat16)


def gather_fsdp(part, axis):
    shards = lax.axis_size("fsdp")
    copies = jnp.broadcast_to(part[None], (shards,) + part.shape)
    got = lax.all_to_all(copies, "fsdp", 0, 0, tiled=False)
    got = jnp.moveaxis(got, 0, axis)
    return got.reshape(part.shape[:axis] + (-1,) + part.shape[axis + 1:])


def body(tokens, grad_out, expert_ids, gate_weights, w_gate, w_up, w_down):
    tok_rows = tokens.shape[0]
    choose = expert_ids.shape[1]
    exp_local = w_gate.shape[0]
    model_width = w_gate.shape[2]
    owners = lax.axis_size("expert")
    experts_all = owners * exp_local
    capacity = max(2, min(tok_rows, 5 * choose * tok_rows // (4 * experts_all)))
    slot_count = experts_all * capacity
    flat_ids = expert_ids.reshape(-1)
    onehot = (flat_ids[:, None] == jnp.arange(experts_all, dtype=jnp.int32)[None, :]).astype(
        jnp.int32
    )
    before = jnp.cumsum(onehot, axis=0) - onehot
    slot_rank = jnp.sum(before * onehot, axis=1)
    slot_of = (flat_ids * capacity + slot_rank).reshape(tok_rows, choose)
    placed = (slot_of[:, :, None] == jnp.arange(slot_count, dtype=jnp.int32)[None, None, :]).astype(
        jnp.float32
    )
    picker = jnp.sum(placed, axis=1).T
    weighted = jnp.einsum("tks,tk->st", placed, gate_weights, precision=lax.Precision.HIGHEST)
    picker_half = picker.astype(jnp.bfloat16)
    scaled_grad = jnp.dot(
        weighted, grad_out.astype(jnp.float32), precision=lax.Precision.HIGHEST
    ).astype(jnp.bfloat16)
    outgoing = jnp.dot(picker_half, tokens, preferred_element_type=jnp.float32).astype(
        jnp.bfloat16
    )
    local_feat = tokens.shape[1]
    both_in = lax.all_to_all(
        jnp.concatenate([outgoing, scaled_grad], axis=1),
        "expert", split_axis=0, concat_axis=0, tiled=True,
    )
    rows_in = lax.all_gather(both_in[:, :local_feat], "fsdp", axis=1, tiled=True)
    grads_in = both_in[:, local_feat:]
    received = rows_in.reshape(owners, exp_local, capacity, model_width)
    cotangent = grads_in.reshape(owners, exp_local, capacity, -1)
    gate_pre = jnp.einsum("jecd,efd->jecf", received, w_gate, preferred_element_type=jnp.float32)
    up_pre = jnp.einsum("jecd,efd->jecf", received, w_up, preferred_element_type=jnp.float32)
    activation, slope_term = silu_parts(gate_pre)
    hidden = (activation * up_pre).astype(jnp.bfloat16)
    hidden_all = gather_fsdp(hidden, 3)
    expert_out = jnp.einsum(
        "jecf,efd->jecd", hidden_all, w_down, preferred_element_type=jnp.float32
    ).astype(jnp.bfloat16)
    shards = lax.axis_size("fsdp")
    exp_n, ff_all, feat = w_down.shape
    hidden_parts = jnp.einsum(
        "jecd,egfd->gjecf", cotangent, w_down.reshape(exp_n, shards, ff_all // shards, feat),
        preferred_element_type=jnp.float32,
    ).astype(jnp.bfloat16)
    grad_hidden = jnp.sum(
        lax.all_to_all(hidden_parts, "fsdp", 0, 0, tiled=False).astype(jnp.float32), axis=0
    )
    grad_gate_pre = (grad_hidden * up_pre * slope_term).astype(jnp.bfloat16)
    grad_up_pre = (grad_hidden * activation).astype(jnp.bfloat16)
    w_gate_g = w_gate.reshape(exp_n, w_gate.shape[1], shards, model_width // shards)
    w_up_g = w_up.reshape(exp_n, w_up.shape[1], shards, model_width // shards)
    input_parts = jnp.einsum(
        "jecf,efgd->gjecd", grad_gate_pre, w_gate_g, preferred_element_type=jnp.float32
    ) + jnp.einsum("jecf,efgd->gjecd", grad_up_pre, w_up_g, preferred_element_type=jnp.float32)
    input_slices = jnp.sum(
        lax.all_to_all(input_parts.astype(jnp.bfloat16), "fsdp", 0, 0, tiled=False).astype(
            jnp.float32
        ),
        axis=0,
    ).astype(jnp.bfloat16)
    grad_gate_w = rounded(
        jnp.einsum("jecf,jecd->efd", grad_gate_pre, received, preferred_element_type=jnp.float32)
    )
    grad_up_w = rounded(
        jnp.einsum("jecf,jecd->efd", grad_up_pre, received, preferred_element_type=jnp.float32)
    )
    grad_down_w = rounded(
        jnp.einsum("jecf,jecd->efd", hidden_all, cotangent, preferred_element_type=jnp.float32)
    )
    gate_up_w, input_slices = lax.optimization_barrier(
        (jnp.stack([grad_gate_w, grad_up_w]).astype(jnp.bfloat16), input_slices)
    )
    summed_gate, summed_up = dp_reduce(gate_up_w, 3).astype(jnp.float32)
    summed_down = dp_reduce(grad_down_w.astype(jnp.bfloat16), 1)
    feat = input_slices.shape[-1]
    both_back = lax.all_to_all(
        jnp.concatenate(
            [expert_out.reshape(slot_count, -1), input_slices.reshape(slot_count, -1)], axis=1
        ),
        "expert", split_axis=0, concat_axis=0, tiled=True,
    )
    mixed_slots, input_slots = both_back[:, :feat], both_back[:, feat:]
    mixed = jnp.dot(
        weighted.T, mixed_slots.astype(jnp.float32), precision=lax.Precision.HIGHEST
    ).astype(jnp.bfloat16)
    grad_tokens = jnp.dot(
        picker.T, input_slots.astype(jnp.float32), precision=lax.Precision.HIGHEST
    ).astype(jnp.bfloat16)
    return (
        mixed,
        grad_tokens,
        summed_gate.astype(jnp.bfloat16),
        summed_up.astype(jnp.bfloat16),
        summed_down,
    )


def solution(mesh):
    in_specs = (
        P(("dp", "expert"), "fsdp"),
        P(("dp", "expert"), "fsdp"),
        P(("dp", "expert"), None),
        P(("dp", "expert"), None),
        P("expert", "fsdp", None),
        P("expert", "fsdp", None),
        P("expert", None, "fsdp"),
    )
    out_specs = (
        P(("dp", "expert"), "fsdp"),
        P(("dp", "expert"), "fsdp"),
        P("expert", "fsdp", "dp"),
        P("expert", "fsdp", "dp"),
        P("expert", "dp", "fsdp"),
    )
    return jax.shard_map(body, mesh=mesh, in_specs=in_specs, out_specs=out_specs, check_vma=False)
```

```python
import jax
import jax.numpy as jnp
from jax import lax
from jax.sharding import PartitionSpec as P


def rounded(values):
    return lax.optimization_barrier(values.astype(jnp.bfloat16)).astype(jnp.float32)


def silu_parts(pre_act):
    sigmoid_value = jax.nn.sigmoid(pre_act)
    return (pre_act * sigmoid_value, sigmoid_value * (1.0 + pre_act * (1.0 - sigmoid_value)))


def dp_reduce(part, axis):
    groups = lax.axis_size("dp")
    if groups != 2:
        return lax.psum_scatter(part, "dp", scatter_dimension=axis, tiled=True)
    me = lax.axis_index("dp")
    halves = jnp.stack(jnp.split(part, 2, axis=axis))
    keep = lax.dynamic_index_in_dim(halves, me, 0, keepdims=False)
    send = lax.dynamic_index_in_dim(halves, 1 - me, 0, keepdims=False)
    got = lax.ppermute(send, "dp", perm=[(0, 1), (1, 0)])
    return (keep.astype(jnp.float32) + got.astype(jnp.float32)).astype(jnp.bfloat16)


def gather_fsdp(part, axis):
    shards = lax.axis_size("fsdp")
    copies = jnp.broadcast_to(part[None], (shards,) + part.shape)
    got = lax.all_to_all(copies, "fsdp", 0, 0, tiled=False)
    got = jnp.moveaxis(got, 0, axis)
    return got.reshape(part.shape[:axis] + (-1,) + part.shape[axis + 1:])


def body(tokens, grad_out, expert_ids, gate_weights, w_gate, w_up, w_down):
    tok_rows = tokens.shape[0]
    choose = expert_ids.shape[1]
    exp_local = w_gate.shape[0]
    model_width = w_gate.shape[2]
    owners = lax.axis_size("expert")
    experts_all = owners * exp_local
    capacity = max(2, min(tok_rows, 5 * choose * tok_rows // (4 * experts_all)))
    slot_count = experts_all * capacity
    flat_ids = expert_ids.reshape(-1)
    onehot = (flat_ids[:, None] == jnp.arange(experts_all, dtype=jnp.int32)[None, :]).astype(
        jnp.int32
    )
    before = jnp.cumsum(onehot, axis=0) - onehot
    slot_rank = jnp.sum(before * onehot, axis=1)
    slot_of = (flat_ids * capacity + slot_rank).reshape(tok_rows, choose)
    placed = (slot_of[:, :, None] == jnp.arange(slot_count, dtype=jnp.int32)[None, None, :]).astype(
        jnp.float32
    )
    picker = jnp.sum(placed, axis=1).T
    weighted = jnp.einsum("tks,tk->st", placed, gate_weights, precision=lax.Precision.HIGHEST)
    picker_half = picker.astype(jnp.bfloat16)
    scaled_grad = jnp.dot(
        weighted, grad_out.astype(jnp.float32), precision=lax.Precision.HIGHEST
    ).astype(jnp.bfloat16)
    outgoing = jnp.dot(picker_half, tokens, preferred_element_type=jnp.float32).astype(
        jnp.bfloat16
    )
    local_feat = tokens.shape[1]
    both_in = lax.all_to_all(
        jnp.concatenate([outgoing, scaled_grad], axis=1),
        "expert", split_axis=0, concat_axis=0, tiled=True,
    )
    rows_in = lax.all_gather(both_in[:, :local_feat], "fsdp", axis=1, tiled=True)
    grads_in = both_in[:, local_feat:]
    received = rows_in.reshape(owners, exp_local, capacity, model_width)
    cotangent = grads_in.reshape(owners, exp_local, capacity, -1)
    gate_pre = jnp.einsum("jecd,efd->jecf", received, w_gate, preferred_element_type=jnp.float32)
    up_pre = jnp.einsum("jecd,efd->jecf", received, w_up, preferred_element_type=jnp.float32)
    activation, slope_term = silu_parts(gate_pre)
    hidden = (activation * up_pre).astype(jnp.bfloat16)
    hidden_all = gather_fsdp(hidden, 3)
    expert_out = jnp.einsum(
        "jecf,efd->jecd", hidden_all, w_down, preferred_element_type=jnp.float32
    ).astype(jnp.bfloat16)
    shards = lax.axis_size("fsdp")
    exp_n, ff_all, feat = w_down.shape
    hidden_parts = jnp.einsum(
        "jecd,egfd->gjecf", cotangent, w_down.reshape(exp_n, shards, ff_all // shards, feat),
        preferred_element_type=jnp.float32,
    ).astype(jnp.bfloat16)
    grad_hidden = jnp.sum(
        lax.all_to_all(hidden_parts, "fsdp", 0, 0, tiled=False).astype(jnp.float32), axis=0
    )
    grad_gate_pre = (grad_hidden * up_pre * slope_term).astype(jnp.bfloat16)
    grad_up_pre = (grad_hidden * activation).astype(jnp.bfloat16)
    w_gate_g = w_gate.reshape(exp_n, w_gate.shape[1], shards, model_width // shards)
    w_up_g = w_up.reshape(exp_n, w_up.shape[1], shards, model_width // shards)
    input_parts = jnp.einsum(
        "jecf,efgd->gjecd", grad_gate_pre, w_gate_g, preferred_element_type=jnp.float32
    ) + jnp.einsum("jecf,efgd->gjecd", grad_up_pre, w_up_g, preferred_element_type=jnp.float32)
    grad_down_w = rounded(
        jnp.einsum("jecf,jecd->efd", hidden_all, cotangent, preferred_element_type=jnp.float32)
    )
    grad_down_w, input_parts = lax.optimization_barrier((grad_down_w, input_parts))
    input_slices = jnp.sum(
        lax.all_to_all(input_parts.astype(jnp.bfloat16), "fsdp", 0, 0, tiled=False).astype(
            jnp.float32
        ),
        axis=0,
    ).astype(jnp.bfloat16)
    feat = input_slices.shape[-1]
    both_back = lax.all_to_all(
        jnp.concatenate(
            [expert_out.reshape(slot_count, -1), input_slices.reshape(slot_count, -1)], axis=1
        ),
        "expert", split_axis=0, concat_axis=0, tiled=True,
    )
    mixed_slots, input_slots = both_back[:, :feat], both_back[:, feat:]
    mixed = jnp.dot(
        weighted.T, mixed_slots.astype(jnp.float32), precision=lax.Precision.HIGHEST
    ).astype(jnp.bfloat16)
    grad_tokens = jnp.dot(
        picker.T, input_slots.astype(jnp.float32), precision=lax.Precision.HIGHEST
    ).astype(jnp.bfloat16)
    grad_gate_w = rounded(
        jnp.einsum("jecf,jecd->efd", grad_gate_pre, received, preferred_element_type=jnp.float32)
    )
    grad_up_w = rounded(
        jnp.einsum("jecf,jecd->efd", grad_up_pre, received, preferred_element_type=jnp.float32)
    )
    summed_gate, summed_up = dp_reduce(
        jnp.stack([grad_gate_w, grad_up_w]).astype(jnp.bfloat16), 3
    ).astype(jnp.float32)
    summed_down = dp_reduce(grad_down_w.astype(jnp.bfloat16), 1)
    return (
        mixed,
        grad_tokens,
        summed_gate.astype(jnp.bfloat16),
        summed_up.astype(jnp.bfloat16),
        summed_down,
    )


def solution(mesh):
    in_specs = (
        P(("dp", "expert"), "fsdp"),
        P(("dp", "expert"), "fsdp"),
        P(("dp", "expert"), None),
        P(("dp", "expert"), None),
        P("expert", "fsdp", None),
        P("expert", "fsdp", None),
        P("expert", None, "fsdp"),
    )
    out_specs = (
        P(("dp", "expert"), "fsdp"),
        P(("dp", "expert"), "fsdp"),
        P("expert", "fsdp", "dp"),
        P("expert", "fsdp", "dp"),
        P("expert", "dp", "fsdp"),
    )
    return jax.shard_map(body, mesh=mesh, in_specs=in_specs, out_specs=out_specs, check_vma=False)
```

```python
import jax
import jax.numpy as jnp
from jax import lax
from jax.sharding import PartitionSpec as P


def rounded(values):
    return lax.optimization_barrier(values.astype(jnp.bfloat16)).astype(jnp.float32)


def silu_parts(pre_act):
    sigmoid_value = jax.nn.sigmoid(pre_act)
    return (pre_act * sigmoid_value, sigmoid_value * (1.0 + pre_act * (1.0 - sigmoid_value)))


def dp_reduce(part, axis):
    groups = lax.axis_size("dp")
    if groups != 2:
        return lax.psum_scatter(part, "dp", scatter_dimension=axis, tiled=True)
    me = lax.axis_index("dp")
    halves = jnp.stack(jnp.split(part, 2, axis=axis))
    keep = lax.dynamic_index_in_dim(halves, me, 0, keepdims=False)
    send = lax.dynamic_index_in_dim(halves, 1 - me, 0, keepdims=False)
    got = lax.ppermute(send, "dp", perm=[(0, 1), (1, 0)])
    return (keep.astype(jnp.float32) + got.astype(jnp.float32)).astype(jnp.bfloat16)


def gather_fsdp(part, axis):
    shards = lax.axis_size("fsdp")
    copies = jnp.broadcast_to(part[None], (shards,) + part.shape)
    got = lax.all_to_all(copies, "fsdp", 0, 0, tiled=False)
    got = jnp.moveaxis(got, 0, axis)
    return got.reshape(part.shape[:axis] + (-1,) + part.shape[axis + 1:])


def body(tokens, grad_out, expert_ids, gate_weights, w_gate, w_up, w_down):
    tok_rows = tokens.shape[0]
    choose = expert_ids.shape[1]
    exp_local = w_gate.shape[0]
    model_width = w_gate.shape[2]
    owners = lax.axis_size("expert")
    experts_all = owners * exp_local
    capacity = max(2, min(tok_rows, 5 * choose * tok_rows // (4 * experts_all)))
    slot_count = experts_all * capacity
    flat_ids = expert_ids.reshape(-1)
    onehot = (flat_ids[:, None] == jnp.arange(experts_all, dtype=jnp.int32)[None, :]).astype(
        jnp.int32
    )
    before = jnp.cumsum(onehot, axis=0) - onehot
    slot_rank = jnp.sum(before * onehot, axis=1)
    slot_of = (flat_ids * capacity + slot_rank).reshape(tok_rows, choose)
    placed = (slot_of[:, :, None] == jnp.arange(slot_count, dtype=jnp.int32)[None, None, :]).astype(
        jnp.float32
    )
    picker = jnp.sum(placed, axis=1).T
    weighted = jnp.einsum("tks,tk->st", placed, gate_weights, precision=lax.Precision.HIGHEST)
    picker_half = picker.astype(jnp.bfloat16)
    scaled_grad = jnp.dot(
        weighted, grad_out.astype(jnp.float32), precision=lax.Precision.HIGHEST
    ).astype(jnp.bfloat16)
    outgoing = jnp.dot(picker_half, tokens, preferred_element_type=jnp.float32).astype(
        jnp.bfloat16
    )
    local_feat = tokens.shape[1]
    both_in = lax.all_to_all(
        jnp.concatenate([outgoing, scaled_grad], axis=1),
        "expert", split_axis=0, concat_axis=0, tiled=True,
    )
    rows_in = lax.all_gather(both_in[:, :local_feat], "fsdp", axis=1, tiled=True)
    grads_in = both_in[:, local_feat:]
    received = rows_in.reshape(owners, exp_local, capacity, model_width)
    cotangent = grads_in.reshape(owners, exp_local, capacity, -1)
    gate_pre = jnp.einsum("jecd,efd->jecf", received, w_gate, preferred_element_type=jnp.float32)
    up_pre = jnp.einsum("jecd,efd->jecf", received, w_up, preferred_element_type=jnp.float32)
    activation, slope_term = silu_parts(gate_pre)
    hidden = (activation * up_pre).astype(jnp.bfloat16)
    hidden_all = gather_fsdp(hidden, 3)
    expert_out = jnp.einsum(
        "jecf,efd->jecd", hidden_all, w_down, preferred_element_type=jnp.float32
    ).astype(jnp.bfloat16)
    shards = lax.axis_size("fsdp")
    exp_n, ff_all, feat = w_down.shape
    hidden_parts = jnp.einsum(
        "jecd,egfd->gjecf", cotangent, w_down.reshape(exp_n, shards, ff_all // shards, feat),
        preferred_element_type=jnp.float32,
    ).astype(jnp.bfloat16)
    grad_hidden = jnp.sum(
        lax.all_to_all(hidden_parts, "fsdp", 0, 0, tiled=False).astype(jnp.float32), axis=0
    )
    grad_gate_pre = (grad_hidden * up_pre * slope_term).astype(jnp.bfloat16)
    grad_up_pre = (grad_hidden * activation).astype(jnp.bfloat16)
    w_gate_g = w_gate.reshape(exp_n, w_gate.shape[1], shards, model_width // shards)
    w_up_g = w_up.reshape(exp_n, w_up.shape[1], shards, model_width // shards)
    input_parts = jnp.einsum(
        "jecf,efgd->gjecd", grad_gate_pre, w_gate_g, preferred_element_type=jnp.float32
    ) + jnp.einsum("jecf,efgd->gjecd", grad_up_pre, w_up_g, preferred_element_type=jnp.float32)
    input_slices = jnp.sum(
        lax.all_to_all(input_parts.astype(jnp.bfloat16), "fsdp", 0, 0, tiled=False).astype(
            jnp.float32
        ),
        axis=0,
    ).astype(jnp.bfloat16)
    feat = input_slices.shape[-1]
    both_back = lax.all_to_all(
        jnp.concatenate(
            [expert_out.reshape(slot_count, -1), input_slices.reshape(slot_count, -1)], axis=1
        ),
        "expert", split_axis=0, concat_axis=0, tiled=True,
    )
    mixed_slots, input_slots = both_back[:, :feat], both_back[:, feat:]
    mixed = jnp.dot(
        weighted.T, mixed_slots.astype(jnp.float32), precision=lax.Precision.HIGHEST
    ).astype(jnp.bfloat16)
    grad_tokens = jnp.dot(
        picker.T, input_slots.astype(jnp.float32), precision=lax.Precision.HIGHEST
    ).astype(jnp.bfloat16)
    grad_gate_w = rounded(
        jnp.einsum("jecf,jecd->efd", grad_gate_pre, received, preferred_element_type=jnp.float32)
    )
    grad_up_w = rounded(
        jnp.einsum("jecf,jecd->efd", grad_up_pre, received, preferred_element_type=jnp.float32)
    )
    grad_down_w = rounded(
        jnp.einsum("jecf,jecd->efd", hidden_all, cotangent, preferred_element_type=jnp.float32)
    )
    summed_gate = dp_reduce(grad_gate_w.astype(jnp.bfloat16), 2).astype(jnp.float32)
    summed_up = dp_reduce(grad_up_w.astype(jnp.bfloat16), 2).astype(jnp.float32)
    summed_down = dp_reduce(grad_down_w.astype(jnp.bfloat16), 1)
    return (
        mixed,
        grad_tokens,
        summed_gate.astype(jnp.bfloat16),
        summed_up.astype(jnp.bfloat16),
        summed_down,
    )


def solution(mesh):
    in_specs = (
        P(("dp", "expert"), "fsdp"),
        P(("dp", "expert"), "fsdp"),
        P(("dp", "expert"), None),
        P(("dp", "expert"), None),
        P("expert", "fsdp", None),
        P("expert", "fsdp", None),
        P("expert", None, "fsdp"),
    )
    out_specs = (
        P(("dp", "expert"), "fsdp"),
        P(("dp", "expert"), "fsdp"),
        P("expert", "fsdp", "dp"),
        P("expert", "fsdp", "dp"),
        P("expert", "dp", "fsdp"),
    )
    return jax.shard_map(body, mesh=mesh, in_specs=in_specs, out_specs=out_specs, check_vma=False)
```
